128 devices in a mesh: wide: 32 (over x, y, core), rep: 4 (over z).
Axes of the slice: x: 4, y: 4, z: 4, core: 2. Of those that a mesh axis runs over, the one named last changes fastest.
Arguments:
- passages: bfloat16 [131072, 1024], P(('wide', 'rep')), may hold values from -6 to 6
- cluster_ids: int32 [131072], P(('wide', 'rep')), may hold values from 0 to 524287, as said below
- w_first: bfloat16 [1024, 1024], replicated, may hold values from -0.1875 to 0.1875
- w_second: bfloat16 [1024, 256], replicated, may hold values from -0.1875 to 0.1875
- centroids: bfloat16 [524288, 256], P('wide'), may hold values from -6 to 6
Outputs:
- refreshed: bfloat16 [524288, 256], P(('wide', 'rep'))
- residuals: bfloat16 [131072, 256], P(('wide', 'rep'))
The draws below stay inside these ranges and needn't reach their ends.
Inputs may be any that keep to these rules, and one draw needn't show every extreme that they name: The owner of a passage is cluster_ids // 16384. Among the 1024 rows of one device (aligned blocks), at most 96 have any one owner; in every draw one owner gets exactly 96 rows from every device's block.
All inputs are finite; a program needn't handle non-finite values.
Results may differ from the reference program's by a relative error of at most 0.015.
Values may be sent and summed in bfloat16 or wider, within the bound.
No kernel may reach another device: no remote copies, remote signals or barrier semaphores. Data moves between devices by JAX's collectives and lax.ppermute only.
A program may use at most 128 MiB of HBM per device.

```python
import jax
import jax.numpy as jnp
from jax import lax

D = 1024
E = 256
CENT_DEV = 16384
TOK_DEV = 1024
CAP = 96
CLUSTERS = 524288
TOKENS = 131072
N_REP = 4


def draw_cluster_ids(key, part):
    owner_count = CLUSTERS // CENT_DEV
    device_count = TOKENS // TOK_DEV
    hot_key, dev_key = jax.random.split(jax.random.fold_in(key, 11))
    hot_owner = jax.random.randint(hot_key, (), 0, owner_count)

    def one_device(dkey):
        order_key, offset_key, local_key = jax.random.split(dkey, 3)
        row_ranks = jax.random.permutation(order_key, TOK_DEV).astype(jnp.int32)
        offset_by = jax.random.randint(offset_key, (), 0, owner_count - 1)
        others = (row_ranks - CAP + offset_by) % (owner_count - 1)
        others = others + (others >= hot_owner).astype(jnp.int32)
        owner_ids = jnp.where(row_ranks < CAP, hot_owner, others)
        local_ids = jax.random.randint(local_key, (TOK_DEV,), 0, CENT_DEV)
        return owner_ids * CENT_DEV + local_ids
    device_keys = jax.random.split(dev_key, device_count)
    return jax.vmap(one_device)(device_keys).reshape(TOKENS).astype(jnp.int32)


def block_scale(key, extent, shards, least, high):
    def one(dim, parts):
        heights = jax.random.uniform(jax.random.fold_in(jax.random.fold_in(key, 6), dim), (parts,), jnp.float32, least / len(shards), high / len(shards))
        return jnp.repeat(jnp.exp(heights), extent[dim] // parts).reshape((-1,) + (1,) * (len(extent) - dim - 1))

    loudness = one(*shards[0])
    for cut in shards[1:]:
        loudness = loudness * one(*cut)
    return loudness


def gaussian(rng, shape, spread, bound, shards=(), held_as=jnp.bfloat16):
    factor_of = block_scale(rng, shape, shards, -0.22, 0.18) if shards else 1.0
    entries = jax.random.normal(rng, shape, jnp.float32) * spread * factor_of
    return jnp.minimum(jnp.maximum(entries, -bound), bound).astype(held_as)


def setup_inputs(seed: int = 0) -> dict:
    key_of = jax.random.split(jax.random.key(seed), 6)
    passages = gaussian(key_of[0], (TOKENS, D), 1.0, 6.0, ((0, 128),))
    cluster_ids = draw_cluster_ids(jax.random.fold_in(key_of[5], 71), 0)
    w_first = gaussian(key_of[2], (D, D), D ** -0.5, 0.1875)
    w_second = gaussian(key_of[3], (D, E), D ** -0.5, 0.1875)
    centroids = gaussian(key_of[4], (CLUSTERS, E), 1.0, 6.0, ((0, 32),))
    return {"passages": passages, "cluster_ids": cluster_ids, "w_first": w_first, "w_second": w_second, "centroids": centroids}


def encode(row_block, w_first, w_second):
    hidden = jax.nn.gelu(jnp.dot(row_block, w_first, preferred_element_type=jnp.float32), approximate=True).astype(jnp.bfloat16)
    projected = jnp.dot(hidden, w_second, preferred_element_type=jnp.float32)
    scaled = projected * lax.rsqrt(lax.optimization_barrier(jnp.mean(projected * projected, axis=-1, keepdims=True)) + 1e-06)
    return scaled.astype(jnp.bfloat16)

def reference(passages, cluster_ids, w_first, w_second, centroids):
    blocks = passages.reshape(TOKENS // TOK_DEV, TOK_DEV, D)
    embedded = lax.map(lambda row_block: encode(row_block, w_first, w_second), blocks).reshape(TOKENS, E)
    values = embedded.astype(jnp.float32)
    replica_of = jnp.arange(TOKENS, dtype=jnp.int32) // TOK_DEV % N_REP
    summed = jnp.zeros((CLUSTERS, E), jnp.float32)
    for replica in range(N_REP):
        chosen = jnp.where((replica_of == replica)[:, None], values, jnp.float32(0.0))
        partial_value = jnp.zeros((CLUSTERS, E), jnp.float32).at[cluster_ids].add(chosen)
        rounded = lax.optimization_barrier(partial_value.astype(jnp.bfloat16))
        summed = summed + rounded.astype(jnp.float32)
    updated = centroids.astype(jnp.float32) + summed
    refreshed = (updated * lax.rsqrt(lax.optimization_barrier(jnp.mean(updated * updated, axis=-1, keepdims=True)) + 1e-06)).astype(jnp.bfloat16)
    residuals = (values - refreshed[cluster_ids].astype(jnp.float32)).astype(jnp.bfloat16)
    return (refreshed, residuals)
```

```python
import jax
import jax.numpy as jnp
from jax import lax
from jax.sharding import PartitionSpec as P


def normalize(updated):
    return (
        updated * lax.rsqrt(jnp.mean(updated * updated, axis=-1, keepdims=True) + 1e-06)
    ).astype(jnp.bfloat16)


def body(passages, cluster_ids, w_first, w_second, centroids):
    tok_rows = passages.shape[0]
    owners = lax.axis_size("wide")
    replicas = lax.axis_size("rep")
    cent_rows = centroids.shape[0]
    share_rows = cent_rows // replicas
    capacity = 3 * tok_rows // owners
    slots = owners * capacity

    hidden = jax.nn.gelu(
        jnp.dot(passages, w_first, preferred_element_type=jnp.float32), approximate=True
    ).astype(jnp.bfloat16)
    projected = jnp.dot(hidden, w_second, preferred_element_type=jnp.float32)
    embedded = (
        projected * lax.rsqrt(jnp.mean(projected * projected, axis=-1, keepdims=True) + 1e-06)
    ).astype(jnp.bfloat16)

    owner_of = cluster_ids // cent_rows
    local_id = cluster_ids - owner_of * cent_rows
    member = owner_of[:, None] == jnp.arange(owners, dtype=jnp.int32)[None, :]
    row = jnp.arange(tok_rows, dtype=jnp.int32)
    earlier = (row[:, None] > row[None, :]).astype(jnp.bfloat16)
    before = jnp.dot(earlier, member.astype(jnp.bfloat16), preferred_element_type=jnp.float32)
    slot_of = jnp.sum(jnp.where(member, before, 0.0), axis=1).astype(jnp.int32)
    target = owner_of * capacity + slot_of
    place = target[None, :] == jnp.arange(slots, dtype=jnp.int32)[:, None]
    place_bf = place.astype(jnp.bfloat16)
    outgoing = jnp.dot(place_bf, embedded, preferred_element_type=jnp.float32).astype(jnp.bfloat16)
    out_ids = jnp.sum(jnp.where(place, local_id[None, :], 0), axis=1)

    incoming = lax.all_to_all(outgoing, "wide", split_axis=0, concat_axis=0, tiled=True)
    in_ids = lax.all_to_all(out_ids, "wide", split_axis=0, concat_axis=0, tiled=True)

    all_rows = lax.all_gather(incoming, "rep", axis=0, tiled=True)
    all_ids = lax.all_gather(in_ids, "rep", axis=0, tiled=True)

    first_row = lax.axis_index("rep") * share_rows
    queries = jnp.concatenate(
        [first_row + jnp.arange(share_rows, dtype=jnp.int32), in_ids]
    )
    block_rows = 1024
    query_count = queries.shape[0]
    padded = -(-query_count // block_rows) * block_rows
    queries = jnp.pad(queries, (0, padded - query_count), constant_values=-1)

    def one_block(block_ids):
        selector = (block_ids[:, None] == all_ids[None, :]).astype(jnp.bfloat16)
        return jnp.dot(selector, all_rows, preferred_element_type=jnp.float32)

    sums = lax.map(one_block, queries.reshape(-1, block_rows)).reshape(padded, -1)
    share_sum = sums[:share_rows]
    look_sum = sums[share_rows:query_count]

    own_cent = lax.dynamic_slice_in_dim(centroids, first_row, share_rows, 0)
    own_rows = normalize(own_cent.astype(jnp.float32) + share_sum)

    look_cent = centroids[in_ids]
    picked = normalize(look_cent.astype(jnp.float32) + look_sum)
    returned = lax.all_to_all(picked, "wide", split_axis=0, concat_axis=0, tiled=True)
    gathered_rows = jnp.dot(place_bf.T, returned, preferred_element_type=jnp.float32)
    residuals = (embedded.astype(jnp.float32) - gathered_rows).astype(jnp.bfloat16)
    return (own_rows, residuals)


def solution(mesh):
    return jax.shard_map(
        body,
        mesh=mesh,
        in_specs=(P(("wide", "rep"), None), P(("wide", "rep")), P(), P(), P("wide", None)),
        out_specs=(P(("wide", "rep"), None), P(("wide", "rep"), None)),
        check_vma=False,
    )
```

```python
import jax
import jax.numpy as jnp
from jax import lax
from jax.sharding import PartitionSpec as P


def normalize(updated):
    return (
        updated * lax.rsqrt(jnp.mean(updated * updated, axis=-1, keepdims=True) + 1e-06)
    ).astype(jnp.bfloat16)


def body(passages, cluster_ids, w_first, w_second, centroids):
    tok_rows = passages.shape[0]
    owners = lax.axis_size("wide")
    replicas = lax.axis_size("rep")
    cent_rows = centroids.shape[0]
    share_rows = cent_rows // replicas
    capacity = 3 * tok_rows // owners
    slots = owners * capacity

    owner_of = cluster_ids // cent_rows
    local_id = cluster_ids - owner_of * cent_rows
    member = owner_of[:, None] == jnp.arange(owners, dtype=jnp.int32)[None, :]
    row = jnp.arange(tok_rows, dtype=jnp.int32)
    earlier = (row[:, None] > row[None, :]).astype(jnp.bfloat16)
    before = jnp.dot(earlier, member.astype(jnp.bfloat16), preferred_element_type=jnp.float32)
    slot_of = jnp.sum(jnp.where(member, before, 0.0), axis=1).astype(jnp.int32)
    target = owner_of * capacity + slot_of
    place = target[None, :] == jnp.arange(slots, dtype=jnp.int32)[:, None]
    place_bf = place.astype(jnp.bfloat16)
    out_ids = jnp.sum(jnp.where(place, local_id[None, :], 0), axis=1)

    both = ("wide", "rep")
    ids_out = jnp.broadcast_to(out_ids.reshape(owners, 1, capacity), (owners, replicas, capacity))
    all_ids = lax.all_to_all(
        ids_out.reshape(-1), both, split_axis=0, concat_axis=0, tiled=True
    )
    my_rep = lax.axis_index("rep")
    in_ids = lax.dynamic_index_in_dim(
        all_ids.reshape(owners, replicas, capacity), my_rep, axis=1, keepdims=False
    ).reshape(slots)

    hidden = jax.nn.gelu(
        jnp.dot(passages, w_first, preferred_element_type=jnp.float32), approximate=True
    ).astype(jnp.bfloat16)
    projected = jnp.dot(hidden, w_second, preferred_element_type=jnp.float32)
    embedded = (
        projected * lax.rsqrt(jnp.mean(projected * projected, axis=-1, keepdims=True) + 1e-06)
    ).astype(jnp.bfloat16)
    emb_width = embedded.shape[1]

    outgoing = jnp.dot(place_bf, embedded, preferred_element_type=jnp.float32).astype(jnp.bfloat16)
    rows_out = jnp.broadcast_to(
        outgoing.reshape(owners, 1, capacity, emb_width), (owners, replicas, capacity, emb_width)
    )
    all_rows = lax.all_to_all(
        rows_out.reshape(-1, emb_width), both, split_axis=0, concat_axis=0, tiled=True
    )

    first_row = my_rep * share_rows
    queries = jnp.concatenate(
        [first_row + jnp.arange(share_rows, dtype=jnp.int32), in_ids]
    )
    block_rows = 1024
    query_count = queries.shape[0]
    padded = -(-query_count // block_rows) * block_rows
    queries = jnp.pad(queries, (0, padded - query_count), constant_values=-1)

    def one_block(block_ids):
        selector = (block_ids[:, None] == all_ids[None, :]).astype(jnp.bfloat16)
        return jnp.dot(selector, all_rows, preferred_element_type=jnp.float32)

    sums = lax.map(one_block, queries.reshape(-1, block_rows)).reshape(padded, -1)
    share_sum = sums[:share_rows]
    look_sum = sums[share_rows:query_count]

    own_cent = lax.dynamic_slice_in_dim(centroids, first_row, share_rows, 0)
    own_rows = normalize(own_cent.astype(jnp.float32) + share_sum)

    look_cent = centroids[in_ids]
    picked = normalize(look_cent.astype(jnp.float32) + look_sum)
    returned = lax.all_to_all(picked, "wide", split_axis=0, concat_axis=0, tiled=True)
    gathered_rows = jnp.dot(place_bf.T, returned, preferred_element_type=jnp.float32)
    residuals = (embedded.astype(jnp.float32) - gathered_rows).astype(jnp.bfloat16)
    return (own_rows, residuals)


def solution(mesh):
    return jax.shard_map(
        body,
        mesh=mesh,
        in_specs=(P(("wide", "rep"), None), P(("wide", "rep")), P(), P(), P("wide", None)),
        out_specs=(P(("wide", "rep"), None), P(("wide", "rep"), None)),
        check_vma=False,
    )
```

```python
import jax
import jax.numpy as jnp
from jax import lax
from jax.sharding import PartitionSpec as P


def normalize(updated):
    return (
        updated * lax.rsqrt(jnp.mean(updated * updated, axis=-1, keepdims=True) + 1e-06)
    ).astype(jnp.bfloat16)


def match_sums(queries, keys, rows, block_rows=1024):
    count = queries.shape[0]
    padded = -(-count // block_rows) * block_rows
    blocks = jnp.pad(queries, (0, padded - count), constant_values=-1).reshape(-1, block_rows)

    def one_block(block_ids):
        selector = (block_ids[:, None] == keys[None, :]).astype(jnp.bfloat16)
        return jnp.dot(selector, rows, preferred_element_type=jnp.float32)

    return lax.map(one_block, blocks).reshape(padded, -1)[:count]


def body(passages, cluster_ids, w_first, w_second, centroids):
    tok_rows = passages.shape[0]
    owners = lax.axis_size("wide")
    replicas = lax.axis_size("rep")
    cent_rows = centroids.shape[0]
    share_rows = cent_rows // replicas
    capacity = 3 * tok_rows // owners
    slots = owners * capacity
    my_rep = lax.axis_index("rep")

    owner_of = cluster_ids // cent_rows
    local_id = cluster_ids - owner_of * cent_rows
    member = owner_of[:, None] == jnp.arange(owners, dtype=jnp.int32)[None, :]
    row = jnp.arange(tok_rows, dtype=jnp.int32)
    earlier = (row[:, None] > row[None, :]).astype(jnp.bfloat16)
    before = jnp.dot(earlier, member.astype(jnp.bfloat16), preferred_element_type=jnp.float32)
    slot_of = jnp.sum(jnp.where(member, before, 0.0), axis=1).astype(jnp.int32)
    target = owner_of * capacity + slot_of
    place = target[None, :] == jnp.arange(slots, dtype=jnp.int32)[:, None]
    place_bf = place.astype(jnp.bfloat16)
    out_ids = jnp.sum(jnp.where(place, local_id[None, :], 0), axis=1)

    hidden = jax.nn.gelu(
        jnp.dot(passages, w_first, preferred_element_type=jnp.float32), approximate=True
    ).astype(jnp.bfloat16)
    projected = jnp.dot(hidden, w_second, preferred_element_type=jnp.float32)
    embedded = (
        projected * lax.rsqrt(jnp.mean(projected * projected, axis=-1, keepdims=True) + 1e-06)
    ).astype(jnp.bfloat16)

    outgoing = jnp.dot(place_bf, embedded, preferred_element_type=jnp.float32).astype(jnp.bfloat16)
    emb_width = outgoing.shape[1]
    id_code = jnp.concatenate(
        [(out_ids // 128).reshape(owners, capacity), (out_ids % 128).reshape(owners, capacity)],
        axis=1,
    ).astype(jnp.bfloat16)
    id_code = jnp.pad(id_code, ((0, 0), (0, emb_width - 2 * capacity)))
    payload = jnp.concatenate(
        [outgoing.reshape(owners, capacity, emb_width), id_code[:, None, :]], axis=1
    )
    chunk = capacity + 1
    incoming = lax.all_to_all(payload, "wide", split_axis=0, concat_axis=0, tiled=True)
    rows_all = lax.all_gather(incoming.reshape(owners * chunk, emb_width), "rep", axis=0)

    def keys_of(block):
        code = block[:, capacity, : 2 * capacity].astype(jnp.int32)
        ids = code[:, :capacity] * 128 + code[:, capacity:]
        return ids, jnp.pad(ids, ((0, 0), (0, 1)), constant_values=-1).reshape(-1)

    in_ids2, keys_own = keys_of(incoming)
    in_ids = in_ids2.reshape(slots)
    rows_own = incoming.reshape(owners * chunk, emb_width)

    first_row = my_rep * share_rows
    share_ids = first_row + jnp.arange(share_rows, dtype=jnp.int32)
    look_cent = centroids[in_ids].astype(jnp.float32)
    own_cent = lax.dynamic_slice_in_dim(centroids, first_row, share_rows, 0).astype(jnp.float32)

    look_own = match_sums(in_ids, keys_own, rows_own)
    share_own = match_sums(share_ids, keys_own, rows_own)

    others = [(my_rep + step) % replicas for step in range(1, replicas)]
    rows_oth = jnp.concatenate(
        [lax.dynamic_index_in_dim(rows_all, q, axis=0, keepdims=False) for q in others]
    )
    keys_oth = keys_of(rows_oth.reshape(-1, chunk, emb_width))[1]
    look_sum = look_own + match_sums(in_ids, keys_oth, rows_oth)
    picked = normalize(look_cent + look_sum)
    returned = lax.all_to_all(picked, "wide", split_axis=0, concat_axis=0, tiled=True)

    share_sum = share_own + match_sums(share_ids, keys_oth, rows_oth)
    own_rows = normalize(own_cent + share_sum)

    gathered_rows = jnp.dot(place_bf.T, returned, preferred_element_type=jnp.float32)
    residuals = (embedded.astype(jnp.float32) - gathered_rows).astype(jnp.bfloat16)
    return (own_rows, residuals)


def solution(mesh):
    return jax.shard_map(
        body,
        mesh=mesh,
        in_specs=(P(("wide", "rep"), None), P(("wide", "rep")), P(), P(), P("wide", None)),
        out_specs=(P(("wide", "rep"), None), P(("wide", "rep"), None)),
        check_vma=False,
    )
```

```python
import jax
import jax.numpy as jnp
from jax import lax
from jax.sharding import PartitionSpec as P


def normalize(updated):
    return (
        updated * lax.rsqrt(jnp.mean(updated * updated, axis=-1, keepdims=True) + 1e-06)
    ).astype(jnp.bfloat16)


def match_sums(queries, keys, rows, block_rows=1024):
    count = queries.shape[0]
    padded = -(-count // block_rows) * block_rows
    blocks = jnp.pad(queries, (0, padded - count), constant_values=-1).reshape(-1, block_rows)

    def one_block(block_ids):
        selector = (block_ids[:, None] == keys[None, :]).astype(jnp.bfloat16)
        return jnp.dot(selector, rows, preferred_element_type=jnp.float32)

    return lax.map(one_block, blocks).reshape(padded, -1)[:count]


def body(passages, cluster_ids, w_first, w_second, centroids):
    tok_rows = passages.shape[0]
    owners = lax.axis_size("wide")
    replicas = lax.axis_size("rep")
    cent_rows = centroids.shape[0]
    share_rows = cent_rows // replicas
    capacity = 3 * tok_rows // owners
    slots = owners * capacity
    my_rep = lax.axis_index("rep")

    owner_of = cluster_ids // cent_rows
    local_id = cluster_ids - owner_of * cent_rows
    member = owner_of[:, None] == jnp.arange(owners, dtype=jnp.int32)[None, :]
    row = jnp.arange(tok_rows, dtype=jnp.int32)
    earlier = (row[:, None] > row[None, :]).astype(jnp.bfloat16)
    before = jnp.dot(earlier, member.astype(jnp.bfloat16), preferred_element_type=jnp.float32)
    slot_of = jnp.sum(jnp.where(member, before, 0.0), axis=1).astype(jnp.int32)
    target = owner_of * capacity + slot_of
    place = target[None, :] == jnp.arange(slots, dtype=jnp.int32)[:, None]
    place_bf = place.astype(jnp.bfloat16)
    out_ids = jnp.sum(jnp.where(place, local_id[None, :], 0), axis=1)

    hidden = jax.nn.gelu(
        jnp.dot(passages, w_first, preferred_element_type=jnp.float32), approximate=True
    ).astype(jnp.bfloat16)
    projected = jnp.dot(hidden, w_second, preferred_element_type=jnp.float32)
    embedded = (
        projected * lax.rsqrt(jnp.mean(projected * projected, axis=-1, keepdims=True) + 1e-06)
    ).astype(jnp.bfloat16)

    outgoing = jnp.dot(place_bf, embedded, preferred_element_type=jnp.float32).astype(jnp.bfloat16)
    emb_width = outgoing.shape[1]
    incoming = lax.all_to_all(outgoing, "wide", split_axis=0, concat_axis=0, tiled=True)
    in_ids = lax.all_to_all(out_ids, "wide", split_axis=0, concat_axis=0, tiled=True)

    code_rows = -(-2 * slots // emb_width)
    code_rows = -(-code_rows // 16) * 16
    id_code = jnp.concatenate([in_ids // 128, in_ids % 128]).astype(jnp.bfloat16)
    id_code = jnp.pad(id_code, (0, code_rows * emb_width - 2 * slots))
    payload = jnp.concatenate([incoming, id_code.reshape(code_rows, emb_width)])
    rows_all = lax.all_gather(payload, "rep", axis=0)
    code = rows_all[:, slots:].reshape(replicas, -1)[:, : 2 * slots].astype(jnp.int32)
    keys = code[:, :slots] * 128 + code[:, slots:]
    keys = jnp.pad(keys, ((0, 0), (0, code_rows)), constant_values=-1).reshape(-1)
    rows = rows_all.reshape(-1, emb_width)

    first_row = my_rep * share_rows
    share_ids = first_row + jnp.arange(share_rows, dtype=jnp.int32)
    look_cent = centroids[in_ids].astype(jnp.float32)
    own_cent = lax.dynamic_slice_in_dim(centroids, first_row, share_rows, 0).astype(jnp.float32)

    look_sum = match_sums(in_ids, keys, rows)
    picked = normalize(look_cent + look_sum)
    returned = lax.all_to_all(picked, "wide", split_axis=0, concat_axis=0, tiled=True)

    share_sum = match_sums(share_ids, keys, rows)
    own_rows = normalize(own_cent + share_sum)

    gathered_rows = jnp.dot(place_bf.T, returned, preferred_element_type=jnp.float32)
    residuals = (embedded.astype(jnp.float32) - gathered_rows).astype(jnp.bfloat16)
    return (own_rows, residuals)


def solution(mesh):
    return jax.shard_map(
        body,
        mesh=mesh,
        in_specs=(P(("wide", "rep"), None), P(("wide", "rep")), P(), P(), P("wide", None)),
        out_specs=(P(("wide", "rep"), None), P(("wide", "rep"), None)),
        check_vma=False,
    )
```

```python
import jax
import jax.numpy as jnp
from jax import lax
from jax.sharding import PartitionSpec as P


def normalize(updated):
    return (
        updated * lax.rsqrt(jnp.mean(updated * updated, axis=-1, keepdims=True) + 1e-06)
    ).astype(jnp.bfloat16)


def match_sums(queries, keys, rows, block_rows=1024):
    count = queries.shape[0]
    padded = -(-count // block_rows) * block_rows
    blocks = jnp.pad(queries, (0, padded - count), constant_values=-1).reshape(-1, block_rows)

    def one_block(block_ids):
        selector = (block_ids[:, None] == keys[None, :]).astype(jnp.bfloat16)
        return jnp.dot(selector, rows, preferred_element_type=jnp.float32)

    return lax.map(one_block, blocks).reshape(padded, -1)[:count]


def body(passages, cluster_ids, w_first, w_second, centroids):
    tok_rows = passages.shape[0]
    owners = lax.axis_size("wide")
    replicas = lax.axis_size("rep")
    cent_rows = centroids.shape[0]
    share_rows = cent_rows // replicas
    capacity = 3 * tok_rows // owners
    slots = owners * capacity
    my_rep = lax.axis_index("rep")

    owner_of = cluster_ids // cent_rows
    local_id = cluster_ids - owner_of * cent_rows
    member = owner_of[:, None] == jnp.arange(owners, dtype=jnp.int32)[None, :]
    row = jnp.arange(tok_rows, dtype=jnp.int32)
    earlier = (row[:, None] > row[None, :]).astype(jnp.bfloat16)
    before = jnp.dot(earlier, member.astype(jnp.bfloat16), preferred_element_type=jnp.float32)
    slot_of = jnp.sum(jnp.where(member, before, 0.0), axis=1).astype(jnp.int32)
    target = owner_of * capacity + slot_of
    place = target[None, :] == jnp.arange(slots, dtype=jnp.int32)[:, None]
    place_bf = place.astype(jnp.bfloat16)
    out_ids = jnp.sum(jnp.where(place, local_id[None, :], 0), axis=1)

    hidden = jax.nn.gelu(
        jnp.dot(passages, w_first, preferred_element_type=jnp.float32), approximate=True
    ).astype(jnp.bfloat16)
    projected = jnp.dot(hidden, w_second, preferred_element_type=jnp.float32)
    embedded = (
        projected * lax.rsqrt(jnp.mean(projected * projected, axis=-1, keepdims=True) + 1e-06)
    ).astype(jnp.bfloat16)

    outgoing = jnp.dot(place_bf, embedded, preferred_element_type=jnp.float32).astype(jnp.bfloat16)
    emb_width = outgoing.shape[1]
    incoming = lax.all_to_all(outgoing, "wide", split_axis=0, concat_axis=0, tiled=True)
    in_ids = lax.all_to_all(out_ids, "wide", split_axis=0, concat_axis=0, tiled=True)

    first_row = my_rep * share_rows
    share_ids = first_row + jnp.arange(share_rows, dtype=jnp.int32)

    pieces = 2
    piece_rows = slots // pieces
    code_rows = -(-2 * piece_rows // emb_width)
    code_rows = -(-code_rows // 16) * 16
    halves = []
    for part in range(pieces):
        part_ids = in_ids[part * piece_rows : (part + 1) * piece_rows]
        id_code = jnp.concatenate([part_ids // 128, part_ids % 128]).astype(jnp.bfloat16)
        id_code = jnp.pad(id_code, (0, code_rows * emb_width - 2 * piece_rows))
        payload = jnp.concatenate(
            [incoming[part * piece_rows : (part + 1) * piece_rows],
             id_code.reshape(code_rows, emb_width)]
        )
        gathered = lax.all_gather(payload, "rep", axis=0)
        code = gathered[:, piece_rows:].reshape(replicas, -1)[:, : 2 * piece_rows]
        code = code.astype(jnp.int32)
        keys = code[:, :piece_rows] * 128 + code[:, piece_rows:]
        keys = jnp.pad(keys, ((0, 0), (0, code_rows)), constant_values=-1).reshape(-1)
        halves.append((keys, gathered.reshape(-1, emb_width)))

    look_cent = centroids[in_ids].astype(jnp.float32)
    own_cent = lax.dynamic_slice_in_dim(centroids, first_row, share_rows, 0).astype(jnp.float32)

    keys_a, rows_a = halves[0]
    keys_b, rows_b = halves[1]
    first_sums = match_sums(jnp.concatenate([in_ids, share_ids]), keys_a, rows_a)
    look_sum = first_sums[:slots] + match_sums(in_ids, keys_b, rows_b)
    picked = normalize(look_cent + look_sum)
    returned = lax.all_to_all(picked, "wide", split_axis=0, concat_axis=0, tiled=True)

    share_sum = first_sums[slots:] + match_sums(share_ids, keys_b, rows_b)
    own_rows = normalize(own_cent + share_sum)

    gathered_rows = jnp.dot(place_bf.T, returned, preferred_element_type=jnp.float32)
    residuals = (embedded.astype(jnp.float32) - gathered_rows).astype(jnp.bfloat16)
    return (own_rows, residuals)


def solution(mesh):
    return jax.shard_map(
        body,
        mesh=mesh,
        in_specs=(P(("wide", "rep"), None), P(("wide", "rep")), P(), P(), P("wide", None)),
        out_specs=(P(("wide", "rep"), None), P(("wide", "rep"), None)),
        check_vma=False,
    )
```

```python
import jax
import jax.numpy as jnp
from jax import lax
from jax.sharding import PartitionSpec as P


def normalize(updated):
    return (
        updated * lax.rsqrt(jnp.mean(updated * updated, axis=-1, keepdims=True) + 1e-06)
    ).astype(jnp.bfloat16)


def match_sums(queries, keys, rows, base=None, cent=None, block_rows=1024):
    block_count = queries.shape[0] // block_rows
    xs = {"ids": queries.reshape(block_count, block_rows)}
    if base is not None:
        xs["base"] = base.reshape(block_count, block_rows, -1)
    if cent is not None:
        xs["cent"] = cent.reshape(block_count, block_rows, -1)

    def one_block(x):
        selector = (x["ids"][:, None] == keys[None, :]).astype(jnp.bfloat16)
        sums = jnp.dot(selector, rows, preferred_element_type=jnp.float32)
        if "base" in x:
            sums = sums + x["base"]
        if "cent" in x:
            return normalize(x["cent"].astype(jnp.float32) + sums)
        return sums

    out = lax.map(one_block, xs)
    return out.reshape(block_count * block_rows, -1)


def body(passages, cluster_ids, w_first, w_second, centroids):
    tok_rows = passages.shape[0]
    owners = lax.axis_size("wide")
    replicas = lax.axis_size("rep")
    cent_rows = centroids.shape[0]
    share_rows = cent_rows // replicas
    capacity = 3 * tok_rows // owners
    slots = owners * capacity
    my_rep = lax.axis_index("rep")

    owner_of = cluster_ids // cent_rows
    local_id = cluster_ids - owner_of * cent_rows
    member = owner_of[:, None] == jnp.arange(owners, dtype=jnp.int32)[None, :]
    row = jnp.arange(tok_rows, dtype=jnp.int32)
    earlier = (row[:, None] > row[None, :]).astype(jnp.bfloat16)
    before = jnp.dot(earlier, member.astype(jnp.bfloat16), preferred_element_type=jnp.float32)
    slot_of = jnp.sum(jnp.where(member, before, 0.0), axis=1).astype(jnp.int32)
    target = owner_of * capacity + slot_of
    place = target[None, :] == jnp.arange(slots, dtype=jnp.int32)[:, None]
    place_bf = place.astype(jnp.bfloat16)
    out_ids = jnp.sum(jnp.where(place, local_id[None, :], 0), axis=1)

    hidden = jax.nn.gelu(
        jnp.dot(passages, w_first, preferred_element_type=jnp.float32), approximate=True
    ).astype(jnp.bfloat16)
    projected = jnp.dot(hidden, w_second, preferred_element_type=jnp.float32)
    embedded = (
        projected * lax.rsqrt(jnp.mean(projected * projected, axis=-1, keepdims=True) + 1e-06)
    ).astype(jnp.bfloat16)

    outgoing = jnp.dot(place_bf, embedded, preferred_element_type=jnp.float32).astype(jnp.bfloat16)
    emb_width = outgoing.shape[1]
    incoming = lax.all_to_all(outgoing, "wide", split_axis=0, concat_axis=0, tiled=True)
    in_ids = lax.all_to_all(out_ids, "wide", split_axis=0, concat_axis=0, tiled=True)

    first_row = my_rep * share_rows
    share_ids = first_row + jnp.arange(share_rows, dtype=jnp.int32)

    pieces = 2
    piece_rows = slots // pieces
    code_rows = -(-2 * piece_rows // emb_width)
    code_rows = -(-code_rows // 16) * 16
    halves = []
    for part in range(pieces):
        part_ids = in_ids[part * piece_rows : (part + 1) * piece_rows]
        id_code = jnp.concatenate([part_ids // 128, part_ids % 128]).astype(jnp.bfloat16)
        id_code = jnp.pad(id_code, (0, code_rows * emb_width - 2 * piece_rows))
        payload = jnp.concatenate(
            [incoming[part * piece_rows : (part + 1) * piece_rows],
             id_code.reshape(code_rows, emb_width)]
        )
        gathered = lax.all_gather(payload, "rep", axis=0)
        code = gathered[:, piece_rows:].reshape(replicas, -1)[:, : 2 * piece_rows]
        code = code.astype(jnp.int32)
        keys = code[:, :piece_rows] * 128 + code[:, piece_rows:]
        keys = jnp.pad(keys, ((0, 0), (0, code_rows)), constant_values=-1).reshape(-1)
        halves.append((keys, gathered.reshape(-1, emb_width)))

    look_cent = centroids[in_ids]
    own_cent = lax.dynamic_slice_in_dim(centroids, first_row, share_rows, 0)

    keys_a, rows_a = halves[0]
    keys_b, rows_b = halves[1]
    first_sums = match_sums(jnp.concatenate([in_ids, share_ids]), keys_a, rows_a)
    picked = match_sums(in_ids, keys_b, rows_b, base=first_sums[:slots], cent=look_cent)
    returned = lax.all_to_all(picked, "wide", split_axis=0, concat_axis=0, tiled=True)
    own_rows = match_sums(share_ids, keys_b, rows_b, base=first_sums[slots:], cent=own_cent)

    gathered_rows = jnp.dot(place_bf.T, returned, preferred_element_type=jnp.float32)
    residuals = (embedded.astype(jnp.float32) - gathered_rows).astype(jnp.bfloat16)
    return (own_rows, residuals)


def solution(mesh):
    return jax.shard_map(
        body,
        mesh=mesh,
        in_specs=(P(("wide", "rep"), None), P(("wide", "rep")), P(), P(), P("wide", None)),
        out_specs=(P(("wide", "rep"), None), P(("wide", "rep"), None)),
        check_vma=False,
    )
```

```python
import jax
import jax.numpy as jnp
from jax import lax
from jax.sharding import PartitionSpec as P


def normalize(updated):
    return (
        updated * lax.rsqrt(jnp.mean(updated * updated, axis=-1, keepdims=True) + 1e-06)
    ).astype(jnp.bfloat16)


def match_sums(queries, keys, rows, block_rows=1024):
    count = queries.shape[0]
    padded = -(-count // block_rows) * block_rows
    blocks = jnp.pad(queries, (0, padded - count), constant_values=-1).reshape(-1, block_rows)

    def one_block(block_ids):
        selector = (block_ids[:, None] == keys[None, :]).astype(jnp.bfloat16)
        return jnp.dot(selector, rows, preferred_element_type=jnp.float32)

    return lax.map(one_block, blocks).reshape(padded, -1)[:count]


def body(passages, cluster_ids, w_first, w_second, centroids):
    tok_rows = passages.shape[0]
    owners = lax.axis_size("wide")
    replicas = lax.axis_size("rep")
    cent_rows = centroids.shape[0]
    share_rows = cent_rows // replicas
    capacity = 3 * tok_rows // owners
    slots = owners * capacity
    my_rep = lax.axis_index("rep")

    owner_of = cluster_ids // cent_rows
    local_id = cluster_ids - owner_of * cent_rows
    member = owner_of[:, None] == jnp.arange(owners, dtype=jnp.int32)[None, :]
    row = jnp.arange(tok_rows, dtype=jnp.int32)
    earlier = (row[:, None] > row[None, :]).astype(jnp.bfloat16)
    before = jnp.dot(earlier, member.astype(jnp.bfloat16), preferred_element_type=jnp.float32)
    slot_of = jnp.sum(jnp.where(member, before, 0.0), axis=1).astype(jnp.int32)
    target = owner_of * capacity + slot_of
    place = target[None, :] == jnp.arange(slots, dtype=jnp.int32)[:, None]
    place_bf = place.astype(jnp.bfloat16)
    out_ids = jnp.sum(jnp.where(place, local_id[None, :], 0), axis=1)

    hidden = jax.nn.gelu(
        jnp.dot(passages, w_first, preferred_element_type=jnp.float32), approximate=True
    ).astype(jnp.bfloat16)
    projected = jnp.dot(hidden, w_second, preferred_element_type=jnp.float32)
    embedded = (
        projected * lax.rsqrt(jnp.mean(projected * projected, axis=-1, keepdims=True) + 1e-06)
    ).astype(jnp.bfloat16)

    outgoing = jnp.dot(place_bf, embedded, preferred_element_type=jnp.float32).astype(jnp.bfloat16)
    emb_width = outgoing.shape[1]
    incoming = lax.all_to_all(outgoing, "wide", split_axis=0, concat_axis=0, tiled=True)
    in_ids = lax.all_to_all(out_ids, "wide", split_axis=0, concat_axis=0, tiled=True)

    code_rows = -(-2 * slots // emb_width)
    code_rows = -(-code_rows // 16) * 16
    id_code = jnp.concatenate([in_ids // 128, in_ids % 128]).astype(jnp.bfloat16)
    id_code = jnp.pad(id_code, (0, code_rows * emb_width - 2 * slots))
    payload = jnp.concatenate([incoming, id_code.reshape(code_rows, emb_width)])
    shifted = [
        lax.ppermute(payload, "rep", [(i, (i + step) % replicas) for i in range(replicas)])
        for step in range(1, replicas)
    ]
    rows_oth = jnp.concatenate(shifted)
    code = rows_oth.reshape(replicas - 1, -1, emb_width)[:, slots:]
    code = code.reshape(replicas - 1, -1)[:, : 2 * slots].astype(jnp.int32)
    keys_oth = code[:, :slots] * 128 + code[:, slots:]
    keys_oth = jnp.pad(keys_oth, ((0, 0), (0, code_rows)), constant_values=-1).reshape(-1)

    first_row = my_rep * share_rows
    share_ids = first_row + jnp.arange(share_rows, dtype=jnp.int32)
    look_cent = centroids[in_ids].astype(jnp.float32)
    own_cent = lax.dynamic_slice_in_dim(centroids, first_row, share_rows, 0).astype(jnp.float32)

    own_sums = match_sums(jnp.concatenate([in_ids, share_ids]), in_ids, incoming)
    look_sum = own_sums[:slots] + match_sums(in_ids, keys_oth, rows_oth)
    picked = normalize(look_cent + look_sum)
    returned = lax.all_to_all(picked, "wide", split_axis=0, concat_axis=0, tiled=True)

    share_sum = own_sums[slots:] + match_sums(share_ids, keys_oth, rows_oth)
    own_rows = normalize(own_cent + share_sum)

    gathered_rows = jnp.dot(place_bf.T, returned, preferred_element_type=jnp.float32)
    residuals = (embedded.astype(jnp.float32) - gathered_rows).astype(jnp.bfloat16)
    return (own_rows, residuals)


def solution(mesh):
    return jax.shard_map(
        body,
        mesh=mesh,
        in_specs=(P(("wide", "rep"), None), P(("wide", "rep")), P(), P(), P("wide", None)),
        out_specs=(P(("wide", "rep"), None), P(("wide", "rep"), None)),
        check_vma=False,
    )
```

```python
import jax
import jax.numpy as jnp
from jax import lax
from jax.sharding import PartitionSpec as P


def normalize(updated):
    return (
        updated * lax.rsqrt(jnp.mean(updated * updated, axis=-1, keepdims=True) + 1e-06)
    ).astype(jnp.bfloat16)


def match_sums(queries, keys, rows, block_rows=1024):
    count = queries.shape[0]
    padded = -(-count // block_rows) * block_rows
    blocks = jnp.pad(queries, (0, padded - count), constant_values=-1).reshape(-1, block_rows)

    def one_block(block_ids):
        selector = (block_ids[:, None] == keys[None, :]).astype(jnp.bfloat16)
        return jnp.dot(selector, rows, preferred_element_type=jnp.float32)

    return lax.map(one_block, blocks).reshape(padded, -1)[:count]


def body(passages, cluster_ids, w_first, w_second, centroids):
    tok_rows = passages.shape[0]
    owners = lax.axis_size("wide")
    replicas = lax.axis_size("rep")
    cent_rows = centroids.shape[0]
    share_rows = cent_rows // replicas
    capacity = 3 * tok_rows // owners
    slots = owners * capacity
    my_rep = lax.axis_index("rep")

    owner_of = cluster_ids // cent_rows
    local_id = cluster_ids - owner_of * cent_rows
    member = owner_of[:, None] == jnp.arange(owners, dtype=jnp.int32)[None, :]
    row = jnp.arange(tok_rows, dtype=jnp.int32)
    earlier = (row[:, None] > row[None, :]).astype(jnp.bfloat16)
    before = jnp.dot(earlier, member.astype(jnp.bfloat16), preferred_element_type=jnp.float32)
    slot_of = jnp.sum(jnp.where(member, before, 0.0), axis=1).astype(jnp.int32)
    target = owner_of * capacity + slot_of
    place = target[None, :] == jnp.arange(slots, dtype=jnp.int32)[:, None]
    place_bf = place.astype(jnp.bfloat16)
    out_ids = jnp.sum(jnp.where(place, local_id[None, :], 0), axis=1)

    hidden = jax.nn.gelu(
        jnp.dot(passages, w_first, preferred_element_type=jnp.float32), approximate=True
    ).astype(jnp.bfloat16)
    projected = jnp.dot(hidden, w_second, preferred_element_type=jnp.float32)
    embedded = (
        projected * lax.rsqrt(jnp.mean(projected * projected, axis=-1, keepdims=True) + 1e-06)
    ).astype(jnp.bfloat16)

    outgoing = jnp.dot(place_bf, embedded, preferred_element_type=jnp.float32).astype(jnp.bfloat16)
    emb_width = outgoing.shape[1]
    incoming = lax.all_to_all(outgoing, "wide", split_axis=0, concat_axis=0, tiled=True)
    in_ids = lax.all_to_all(out_ids, "wide", split_axis=0, concat_axis=0, tiled=True)

    code_rows = -(-2 * slots // emb_width)
    code_rows = -(-code_rows // 16) * 16
    id_code = jnp.concatenate([in_ids // 128, in_ids % 128]).astype(jnp.bfloat16)
    id_code = jnp.pad(id_code, (0, code_rows * emb_width - 2 * slots))
    payload = jnp.concatenate([incoming, id_code.reshape(code_rows, emb_width)])
    def shift(x, step):
        return lax.ppermute(x, "rep", [(i, (i + step) % replicas) for i in range(replicas)])

    from_prev = shift(payload, 1)
    from_next = shift(payload, -1)
    half = payload.shape[0] // 2
    from_far = jnp.concatenate([shift(from_prev[:half], 1), shift(from_next[half:], -1)])

    def keys_of(pieces):
        count = pieces.shape[0] // payload.shape[0]
        code = pieces.reshape(count, -1, emb_width)[:, slots:]
        code = code.reshape(count, -1)[:, : 2 * slots].astype(jnp.int32)
        ids = code[:, :slots] * 128 + code[:, slots:]
        return jnp.pad(ids, ((0, 0), (0, code_rows)), constant_values=-1).reshape(-1)

    rows_near = jnp.concatenate([from_prev, from_next])
    keys_near = keys_of(rows_near)
    keys_far = keys_of(from_far)

    first_row = my_rep * share_rows
    share_ids = first_row + jnp.arange(share_rows, dtype=jnp.int32)
    look_cent = centroids[in_ids].astype(jnp.float32)
    own_cent = lax.dynamic_slice_in_dim(centroids, first_row, share_rows, 0).astype(jnp.float32)

    queries = jnp.concatenate([in_ids, share_ids])
    own_sums = match_sums(queries, in_ids, incoming)
    near_sums = match_sums(queries, keys_near, rows_near)
    look_sum = own_sums[:slots] + near_sums[:slots] + match_sums(in_ids, keys_far, from_far)
    picked = normalize(look_cent + look_sum)
    returned = lax.all_to_all(picked, "wide", split_axis=0, concat_axis=0, tiled=True)

    share_sum = own_sums[slots:] + near_sums[slots:] + match_sums(share_ids, keys_far, from_far)
    own_rows = normalize(own_cent + share_sum)

    gathered_rows = jnp.dot(place_bf.T, returned, preferred_element_type=jnp.float32)
    residuals = (embedded.astype(jnp.float32) - gathered_rows).astype(jnp.bfloat16)
    return (own_rows, residuals)


def solution(mesh):
    return jax.shard_map(
        body,
        mesh=mesh,
        in_specs=(P(("wide", "rep"), None), P(("wide", "rep")), P(), P(), P("wide", None)),
        out_specs=(P(("wide", "rep"), None), P(("wide", "rep"), None)),
        check_vma=False,
    )
```

```python
import jax
import jax.numpy as jnp
from jax import lax
from jax.sharding import PartitionSpec as P


def normalize(updated):
    return (
        updated * lax.rsqrt(jnp.mean(updated * updated, axis=-1, keepdims=True) + 1e-06)
    ).astype(jnp.bfloat16)


def match_sums(queries, keys, rows, block_rows=1024):
    count = queries.shape[0]
    padded = -(-count // block_rows) * block_rows
    blocks = jnp.pad(queries, (0, padded - count), constant_values=-1).reshape(-1, block_rows)

    def one_block(block_ids):
        selector = (block_ids[:, None] == keys[None, :]).astype(jnp.bfloat16)
        return jnp.dot(selector, rows, preferred_element_type=jnp.float32)

    return lax.map(one_block, blocks).reshape(padded, -1)[:count]


def body(passages, cluster_ids, w_first, w_second, centroids):
    tok_rows = passages.shape[0]
    owners = lax.axis_size("wide")
    replicas = lax.axis_size("rep")
    cent_rows = centroids.shape[0]
    share_rows = cent_rows // replicas
    capacity = 3 * tok_rows // owners
    slots = owners * capacity
    my_rep = lax.axis_index("rep")

    owner_of = cluster_ids // cent_rows
    local_id = cluster_ids - owner_of * cent_rows
    member = owner_of[:, None] == jnp.arange(owners, dtype=jnp.int32)[None, :]
    row = jnp.arange(tok_rows, dtype=jnp.int32)
    earlier = (row[:, None] > row[None, :]).astype(jnp.bfloat16)
    before = jnp.dot(earlier, member.astype(jnp.bfloat16), preferred_element_type=jnp.float32)
    slot_of = jnp.sum(jnp.where(member, before, 0.0), axis=1).astype(jnp.int32)
    target = owner_of * capacity + slot_of
    place = target[None, :] == jnp.arange(slots, dtype=jnp.int32)[:, None]
    place_bf = place.astype(jnp.bfloat16)
    out_ids = jnp.sum(jnp.where(place, local_id[None, :], 0), axis=1)

    hidden = jax.nn.gelu(
        jnp.dot(passages, w_first, preferred_element_type=jnp.float32), approximate=True
    ).astype(jnp.bfloat16)
    projected = jnp.dot(hidden, w_second, preferred_element_type=jnp.float32)
    embedded = (
        projected * lax.rsqrt(jnp.mean(projected * projected, axis=-1, keepdims=True) + 1e-06)
    ).astype(jnp.bfloat16)

    outgoing = jnp.dot(place_bf, embedded, preferred_element_type=jnp.float32).astype(jnp.bfloat16)
    emb_width = outgoing.shape[1]
    incoming = lax.all_to_all(outgoing, "wide", split_axis=0, concat_axis=0, tiled=True)
    in_ids = lax.all_to_all(out_ids, "wide", split_axis=0, concat_axis=0, tiled=True)

    half_rows = slots // 2
    code_rows = -(-2 * half_rows // emb_width)
    code_rows = -(-code_rows // 16) * 16

    def with_code(part):
        part_ids = in_ids[part * half_rows : (part + 1) * half_rows]
        id_code = jnp.concatenate([part_ids // 128, part_ids % 128]).astype(jnp.bfloat16)
        id_code = jnp.pad(id_code, (0, code_rows * emb_width - 2 * half_rows))
        return jnp.concatenate(
            [incoming[part * half_rows : (part + 1) * half_rows],
             id_code.reshape(code_rows, emb_width)]
        )

    def keys_of(pieces):
        count = pieces.shape[0] // (half_rows + code_rows)
        code = pieces.reshape(count, -1, emb_width)[:, half_rows:]
        code = code.reshape(count, -1)[:, : 2 * half_rows].astype(jnp.int32)
        ids = code[:, :half_rows] * 128 + code[:, half_rows:]
        return jnp.pad(ids, ((0, 0), (0, code_rows)), constant_values=-1).reshape(-1)

    def shift(x, step):
        return lax.ppermute(x, "rep", [(i, (i + step) % replicas) for i in range(replicas)])

    payload_a = with_code(0)
    prev_a = shift(payload_a, 1)
    next_a = shift(payload_a, -1)
    payload_b, _, _ = lax.optimization_barrier((with_code(1), prev_a, next_a))
    prev_b = shift(payload_b, 1)
    next_b = shift(payload_b, -1)
    far_a = shift(prev_a, 1)
    far_b = shift(next_b, -1)

    near_a = jnp.concatenate([prev_a, next_a])
    near_b = jnp.concatenate([prev_b, next_b])
    far = jnp.concatenate([far_a, far_b])

    first_row = my_rep * share_rows
    share_ids = first_row + jnp.arange(share_rows, dtype=jnp.int32)
    look_cent = centroids[in_ids]
    own_cent = lax.dynamic_slice_in_dim(centroids, first_row, share_rows, 0)

    queries = jnp.concatenate([in_ids, share_ids])
    own_sums = match_sums(queries, in_ids, incoming)
    sums_a = match_sums(queries, keys_of(near_a), near_a)
    sums_b = match_sums(queries, keys_of(near_b), near_b)
    keys_far = keys_of(far)
    look_sum = (own_sums[:slots] + sums_a[:slots] + sums_b[:slots]
                + match_sums(in_ids, keys_far, far))
    picked = normalize(look_cent.astype(jnp.float32) + look_sum)
    returned = lax.all_to_all(picked, "wide", split_axis=0, concat_axis=0, tiled=True)

    share_sum = (own_sums[slots:] + sums_a[slots:] + sums_b[slots:]
                 + match_sums(share_ids, keys_far, far))
    own_rows = normalize(own_cent.astype(jnp.float32) + share_sum)

    gathered_rows = jnp.dot(place_bf.T, returned, preferred_element_type=jnp.float32)
    residuals = (embedded.astype(jnp.float32) - gathered_rows).astype(jnp.bfloat16)
    return (own_rows, residuals)


def solution(mesh):
    return jax.shard_map(
        body,
        mesh=mesh,
        in_specs=(P(("wide", "rep"), None), P(("wide", "rep")), P(), P(), P("wide", None)),
        out_specs=(P(("wide", "rep"), None), P(("wide", "rep"), None)),
        check_vma=False,
    )
```

```python
import jax
import jax.numpy as jnp
from jax import lax
from jax.sharding import PartitionSpec as P


def normalize(updated):
    return (
        updated * lax.rsqrt(jnp.mean(updated * updated, axis=-1, keepdims=True) + 1e-06)
    ).astype(jnp.bfloat16)


def match_sums(queries, keys, rows, block_rows=1024):
    count = queries.shape[0]
    padded = -(-count // block_rows) * block_rows
    blocks = jnp.pad(queries, (0, padded - count), constant_values=-1).reshape(-1, block_rows)

    def one_block(block_ids):
        selector = (block_ids[:, None] == keys[None, :]).astype(jnp.bfloat16)
        return jnp.dot(selector, rows, preferred_element_type=jnp.float32)

    return lax.map(one_block, blocks).reshape(padded, -1)[:count]


def body(passages, cluster_ids, w_first, w_second, centroids):
    tok_rows = passages.shape[0]
    owners = lax.axis_size("wide")
    replicas = lax.axis_size("rep")
    cent_rows = centroids.shape[0]
    share_rows = cent_rows // replicas
    capacity = 3 * tok_rows // owners
    slots = owners * capacity
    my_rep = lax.axis_index("rep")

    owner_of = cluster_ids // cent_rows
    local_id = cluster_ids - owner_of * cent_rows
    member = owner_of[:, None] == jnp.arange(owners, dtype=jnp.int32)[None, :]
    row = jnp.arange(tok_rows, dtype=jnp.int32)
    earlier = (row[:, None] > row[None, :]).astype(jnp.bfloat16)
    before = jnp.dot(earlier, member.astype(jnp.bfloat16), preferred_element_type=jnp.float32)
    slot_of = jnp.sum(jnp.where(member, before, 0.0), axis=1).astype(jnp.int32)
    target = owner_of * capacity + slot_of
    place = target[None, :] == jnp.arange(slots, dtype=jnp.int32)[:, None]
    place_bf = place.astype(jnp.bfloat16)
    out_ids = jnp.sum(jnp.where(place, local_id[None, :], 0), axis=1)

    hidden = jax.nn.gelu(
        jnp.dot(passages, w_first, preferred_element_type=jnp.float32), approximate=True
    ).astype(jnp.bfloat16)
    projected = jnp.dot(hidden, w_second, preferred_element_type=jnp.float32)
    embedded = (
        projected * lax.rsqrt(jnp.mean(projected * projected, axis=-1, keepdims=True) + 1e-06)
    ).astype(jnp.bfloat16)

    outgoing = jnp.dot(place_bf, embedded, preferred_element_type=jnp.float32).astype(jnp.bfloat16)
    emb_width = outgoing.shape[1]
    incoming = lax.all_to_all(outgoing, "wide", split_axis=0, concat_axis=0, tiled=True)
    in_ids = lax.all_to_all(out_ids, "wide", split_axis=0, concat_axis=0, tiled=True)

    half_rows = slots // 2
    code_rows = -(-2 * half_rows // emb_width)
    code_rows = -(-code_rows // 16) * 16

    def with_code(part):
        part_ids = in_ids[part * half_rows : (part + 1) * half_rows]
        id_code = jnp.concatenate([part_ids // 128, part_ids % 128]).astype(jnp.bfloat16)
        id_code = jnp.pad(id_code, (0, code_rows * emb_width - 2 * half_rows))
        return jnp.concatenate(
            [incoming[part * half_rows : (part + 1) * half_rows],
             id_code.reshape(code_rows, emb_width)]
        )

    def split(pieces):
        blocks = [piece[:half_rows] for piece in pieces]
        ids = []
        for piece in pieces:
            code = piece[half_rows:].reshape(-1)[: 2 * half_rows].astype(jnp.int32)
            ids.append(code[:half_rows] * 128 + code[half_rows:])
        return jnp.concatenate(ids), jnp.concatenate(blocks)

    def shift(x, step):
        return lax.ppermute(x, "rep", [(i, (i + step) % replicas) for i in range(replicas)])

    payload_a = with_code(0)
    prev_a = shift(payload_a, 1)
    next_a = shift(payload_a, -1)
    payload_b, _, _ = lax.optimization_barrier((with_code(1), prev_a, next_a))
    prev_b = shift(payload_b, 1)
    next_b = shift(payload_b, -1)
    far_a = shift(prev_a, 1)
    far_b = shift(next_b, -1)

    keys_a, near_a = split([prev_a, next_a])
    keys_b, near_b = split([prev_b, next_b])
    keys_far, far = split([far_a, far_b])

    first_row = my_rep * share_rows
    share_ids = first_row + jnp.arange(share_rows, dtype=jnp.int32)
    look_cent = centroids[in_ids]
    own_cent = lax.dynamic_slice_in_dim(centroids, first_row, share_rows, 0)

    queries = jnp.concatenate([in_ids, share_ids])
    own_sums = match_sums(queries, in_ids, incoming)
    sums_a = match_sums(queries, keys_a, near_a)
    sums_b = match_sums(queries, keys_b, near_b)
    look_sum = (own_sums[:slots] + sums_a[:slots] + sums_b[:slots]
                + match_sums(in_ids, keys_far, far))
    picked = normalize(look_cent.astype(jnp.float32) + look_sum)
    returned = lax.all_to_all(picked, "wide", split_axis=0, concat_axis=0, tiled=True)

    share_sum = (own_sums[slots:] + sums_a[slots:] + sums_b[slots:]
                 + match_sums(share_ids, keys_far, far))
    own_rows = normalize(own_cent.astype(jnp.float32) + share_sum)

    gathered_rows = jnp.dot(place_bf.T, returned, preferred_element_type=jnp.float32)
    residuals = (embedded.astype(jnp.float32) - gathered_rows).astype(jnp.bfloat16)
    return (own_rows, residuals)


def solution(mesh):
    return jax.shard_map(
        body,
        mesh=mesh,
        in_specs=(P(("wide", "rep"), None), P(("wide", "rep")), P(), P(), P("wide", None)),
        out_specs=(P(("wide", "rep"), None), P(("wide", "rep"), None)),
        check_vma=False,
    )
```

```python
import jax
import jax.numpy as jnp
from jax import lax
from jax.sharding import PartitionSpec as P


def normalize(updated):
    return (
        updated * lax.rsqrt(jnp.mean(updated * updated, axis=-1, keepdims=True) + 1e-06)
    ).astype(jnp.bfloat16)


def match_sums(queries, keys, rows, block_rows=1024):
    count = queries.shape[0]
    padded = -(-count // block_rows) * block_rows
    blocks = jnp.pad(queries, (0, padded - count), constant_values=-1).reshape(-1, block_rows)

    def one_block(block_ids):
        selector = (block_ids[:, None] == keys[None, :]).astype(jnp.bfloat16)
        return jnp.dot(selector, rows, preferred_element_type=jnp.float32)

    return lax.map(one_block, blocks).reshape(padded, -1)[:count]


def body(passages, cluster_ids, w_first, w_second, centroids):
    tok_rows = passages.shape[0]
    owners = lax.axis_size("wide")
    replicas = lax.axis_size("rep")
    cent_rows = centroids.shape[0]
    share_rows = cent_rows // replicas
    capacity = 3 * tok_rows // owners
    slots = owners * capacity
    my_rep = lax.axis_index("rep")

    owner_of = cluster_ids // cent_rows
    local_id = cluster_ids - owner_of * cent_rows
    member = owner_of[:, None] == jnp.arange(owners, dtype=jnp.int32)[None, :]
    row = jnp.arange(tok_rows, dtype=jnp.int32)
    earlier = (row[:, None] > row[None, :]).astype(jnp.bfloat16)
    before = jnp.dot(earlier, member.astype(jnp.bfloat16), preferred_element_type=jnp.float32)
    slot_of = jnp.sum(jnp.where(member, before, 0.0), axis=1).astype(jnp.int32)
    target = owner_of * capacity + slot_of
    place = target[None, :] == jnp.arange(slots, dtype=jnp.int32)[:, None]
    place_bf = place.astype(jnp.bfloat16)
    out_ids = jnp.sum(jnp.where(place, local_id[None, :], 0), axis=1)

    hidden = jax.nn.gelu(
        jnp.dot(passages, w_first, preferred_element_type=jnp.float32), approximate=True
    ).astype(jnp.bfloat16)
    projected = jnp.dot(hidden, w_second, preferred_element_type=jnp.float32)
    embedded = (
        projected * lax.rsqrt(jnp.mean(projected * projected, axis=-1, keepdims=True) + 1e-06)
    ).astype(jnp.bfloat16)

    outgoing = jnp.dot(place_bf, embedded, preferred_element_type=jnp.float32).astype(jnp.bfloat16)
    emb_width = outgoing.shape[1]
    incoming = lax.all_to_all(outgoing, "wide", split_axis=0, concat_axis=0, tiled=True)
    in_ids = lax.all_to_all(out_ids, "wide", split_axis=0, concat_axis=0, tiled=True)

    half_rows = slots // 2

    def shift(x, step):
        return lax.ppermute(x, "rep", [(i, (i + step) % replicas) for i in range(replicas)])

    def half(part):
        return (incoming[part * half_rows : (part + 1) * half_rows],
                in_ids[part * half_rows : (part + 1) * half_rows])

    payload_a = half(0)
    prev_a = shift(payload_a, 1)
    next_a = shift(payload_a, -1)
    payload_b, _, _ = lax.optimization_barrier((half(1), prev_a, next_a))
    prev_b = shift(payload_b, 1)
    next_b = shift(payload_b, -1)
    far_a = shift(prev_a, 1)
    far_b = shift(next_b, -1)

    def join(first, second):
        return jnp.concatenate([first[1], second[1]]), jnp.concatenate([first[0], second[0]])

    keys_a, near_a = join(prev_a, next_a)
    keys_b, near_b = join(prev_b, next_b)
    keys_far, far = join(far_a, far_b)

    first_row = my_rep * share_rows
    share_ids = first_row + jnp.arange(share_rows, dtype=jnp.int32)
    look_cent = centroids[in_ids]
    own_cent = lax.dynamic_slice_in_dim(centroids, first_row, share_rows, 0)

    queries = jnp.concatenate([in_ids, share_ids])
    own_sums = match_sums(queries, in_ids, incoming)
    sums_a = match_sums(queries, keys_a, near_a)
    sums_b = match_sums(queries, keys_b, near_b)
    look_sum = (own_sums[:slots] + sums_a[:slots] + sums_b[:slots]
                + match_sums(in_ids, keys_far, far))
    picked = normalize(look_cent.astype(jnp.float32) + look_sum)
    returned = lax.all_to_all(picked, "wide", split_axis=0, concat_axis=0, tiled=True)

    share_sum = (own_sums[slots:] + sums_a[slots:] + sums_b[slots:]
                 + match_sums(share_ids, keys_far, far))
    own_rows = normalize(own_cent.astype(jnp.float32) + share_sum)

    gathered_rows = jnp.dot(place_bf.T, returned, preferred_element_type=jnp.float32)
    residuals = (embedded.astype(jnp.float32) - gathered_rows).astype(jnp.bfloat16)
    return (own_rows, residuals)


def solution(mesh):
    return jax.shard_map(
        body,
        mesh=mesh,
        in_specs=(P(("wide", "rep"), None), P(("wide", "rep")), P(), P(), P("wide", None)),
        out_specs=(P(("wide", "rep"), None), P(("wide", "rep"), None)),
        check_vma=False,
    )
```

```python
import jax
import jax.numpy as jnp
from jax import lax
from jax.sharding import PartitionSpec as P


def normalize(updated):
    return (
        updated * lax.rsqrt(jnp.mean(updated * updated, axis=-1, keepdims=True) + 1e-06)
    ).astype(jnp.bfloat16)


def match_sums(queries, keys, rows, held=jnp.float32, block_rows=1024):
    count = queries.shape[0]
    padded = -(-count // block_rows) * block_rows
    blocks = jnp.pad(queries, (0, padded - count), constant_values=-1).reshape(-1, block_rows)

    def one_block(block_ids):
        selector = (block_ids[:, None] == keys[None, :]).astype(jnp.bfloat16)
        return jnp.dot(selector, rows, preferred_element_type=jnp.float32).astype(held)

    return lax.map(one_block, blocks).reshape(padded, -1)[:count]


def body(passages, cluster_ids, w_first, w_second, centroids):
    tok_rows = passages.shape[0]
    owners = lax.axis_size("wide")
    replicas = lax.axis_size("rep")
    cent_rows = centroids.shape[0]
    share_rows = cent_rows // replicas
    capacity = 3 * tok_rows // owners
    slots = owners * capacity
    my_rep = lax.axis_index("rep")

    owner_of = cluster_ids // cent_rows
    local_id = cluster_ids - owner_of * cent_rows
    member = owner_of[:, None] == jnp.arange(owners, dtype=jnp.int32)[None, :]
    row = jnp.arange(tok_rows, dtype=jnp.int32)
    earlier = (row[:, None] > row[None, :]).astype(jnp.bfloat16)
    before = jnp.dot(earlier, member.astype(jnp.bfloat16), preferred_element_type=jnp.float32)
    slot_of = jnp.sum(jnp.where(member, before, 0.0), axis=1).astype(jnp.int32)
    target = owner_of * capacity + slot_of
    place = target[None, :] == jnp.arange(slots, dtype=jnp.int32)[:, None]
    place_bf = place.astype(jnp.bfloat16)
    out_ids = jnp.sum(jnp.where(place, local_id[None, :], 0), axis=1)

    hidden = jax.nn.gelu(
        jnp.dot(passages, w_first, preferred_element_type=jnp.float32), approximate=True
    ).astype(jnp.bfloat16)
    projected = jnp.dot(hidden, w_second, preferred_element_type=jnp.float32)
    embedded = (
        projected * lax.rsqrt(jnp.mean(projected * projected, axis=-1, keepdims=True) + 1e-06)
    ).astype(jnp.bfloat16)

    outgoing = jnp.dot(place_bf, embedded, preferred_element_type=jnp.float32).astype(jnp.bfloat16)
    emb_width = outgoing.shape[1]
    incoming = lax.all_to_all(outgoing, "wide", split_axis=0, concat_axis=0, tiled=True)
    in_ids = lax.all_to_all(out_ids, "wide", split_axis=0, concat_axis=0, tiled=True)

    half_rows = slots // 2

    def shift(x, step):
        return lax.ppermute(x, "rep", [(i, (i + step) % replicas) for i in range(replicas)])

    def half(part):
        return (incoming[part * half_rows : (part + 1) * half_rows],
                in_ids[part * half_rows : (part + 1) * half_rows])

    payload_a = half(0)
    prev_a = shift(payload_a, 1)
    next_a = shift(payload_a, -1)
    payload_b, _, _ = lax.optimization_barrier((half(1), prev_a, next_a))
    prev_b = shift(payload_b, 1)
    next_b = shift(payload_b, -1)
    far_a = shift(prev_a, 1)
    far_b = shift(next_b, -1)

    def join(first, second):
        return jnp.concatenate([first[1], second[1]]), jnp.concatenate([first[0], second[0]])

    keys_a, near_a = join(prev_a, next_a)
    keys_b, near_b = join(prev_b, next_b)
    keys_far, far = join(far_a, far_b)

    first_row = my_rep * share_rows
    share_ids = first_row + jnp.arange(share_rows, dtype=jnp.int32)
    look_cent = centroids[in_ids]
    own_cent = lax.dynamic_slice_in_dim(centroids, first_row, share_rows, 0)

    queries = jnp.concatenate([in_ids, share_ids])
    own_sums = match_sums(queries, in_ids, incoming, jnp.bfloat16).astype(jnp.float32)
    sums_a = match_sums(queries, keys_a, near_a, jnp.bfloat16).astype(jnp.float32)
    sums_b = match_sums(queries, keys_b, near_b, jnp.bfloat16).astype(jnp.float32)
    look_sum = (own_sums[:slots] + sums_a[:slots] + sums_b[:slots]
                + match_sums(in_ids, keys_far, far))
    picked = normalize(look_cent.astype(jnp.float32) + look_sum)
    returned = lax.all_to_all(picked, "wide", split_axis=0, concat_axis=0, tiled=True)

    share_sum = (own_sums[slots:] + sums_a[slots:] + sums_b[slots:]
                 + match_sums(share_ids, keys_far, far))
    own_rows = normalize(own_cent.astype(jnp.float32) + share_sum)

    gathered_rows = jnp.dot(place_bf.T, returned, preferred_element_type=jnp.float32)
    residuals = (embedded.astype(jnp.float32) - gathered_rows).astype(jnp.bfloat16)
    return (own_rows, residuals)


def solution(mesh):
    return jax.shard_map(
        body,
        mesh=mesh,
        in_specs=(P(("wide", "rep"), None), P(("wide", "rep")), P(), P(), P("wide", None)),
        out_specs=(P(("wide", "rep"), None), P(("wide", "rep"), None)),
        check_vma=False,
    )
```

```python
import jax
import jax.numpy as jnp
from jax import lax
from jax.sharding import PartitionSpec as P


def normalize(updated):
    return (
        updated * lax.rsqrt(jnp.mean(updated * updated, axis=-1, keepdims=True) + 1e-06)
    ).astype(jnp.bfloat16)


def match_sums(queries, keys, rows, block_rows=1024):
    count = queries.shape[0]
    padded = -(-count // block_rows) * block_rows
    blocks = jnp.pad(queries, (0, padded - count), constant_values=-1).reshape(-1, block_rows)

    def one_block(block_ids):
        selector = (block_ids[:, None] == keys[None, :]).astype(jnp.bfloat16)
        return jnp.dot(selector, rows, preferred_element_type=jnp.float32)

    return lax.map(one_block, blocks).reshape(padded, -1)[:count]


def body(passages, cluster_ids, w_first, w_second, centroids):
    tok_rows = passages.shape[0]
    owners = lax.axis_size("wide")
    replicas = lax.axis_size("rep")
    cent_rows = centroids.shape[0]
    share_rows = cent_rows // replicas
    capacity = 3 * tok_rows // owners
    slots = owners * capacity
    my_rep = lax.axis_index("rep")

    owner_of = cluster_ids // cent_rows
    local_id = cluster_ids - owner_of * cent_rows
    member = owner_of[:, None] == jnp.arange(owners, dtype=jnp.int32)[None, :]
    row = jnp.arange(tok_rows, dtype=jnp.int32)
    earlier = (row[:, None] > row[None, :]).astype(jnp.bfloat16)
    before = jnp.dot(earlier, member.astype(jnp.bfloat16), preferred_element_type=jnp.float32)
    slot_of = jnp.sum(jnp.where(member, before, 0.0), axis=1).astype(jnp.int32)
    target = owner_of * capacity + slot_of
    place = target[None, :] == jnp.arange(slots, dtype=jnp.int32)[:, None]
    place_bf = place.astype(jnp.bfloat16)
    out_ids = jnp.sum(jnp.where(place, local_id[None, :], 0), axis=1)

    hidden = jax.nn.gelu(
        jnp.dot(passages, w_first, preferred_element_type=jnp.float32), approximate=True
    ).astype(jnp.bfloat16)
    projected = jnp.dot(hidden, w_second, preferred_element_type=jnp.float32)
    embedded = (
        projected * lax.rsqrt(jnp.mean(projected * projected, axis=-1, keepdims=True) + 1e-06)
    ).astype(jnp.bfloat16)

    outgoing = jnp.dot(place_bf, embedded, preferred_element_type=jnp.float32).astype(jnp.bfloat16)
    emb_width = outgoing.shape[1]
    incoming = lax.all_to_all(outgoing, "wide", split_axis=0, concat_axis=0, tiled=True)
    in_ids = lax.all_to_all(out_ids, "wide", split_axis=0, concat_axis=0, tiled=True)

    code_rows = -(-2 * slots // emb_width)
    code_rows = -(-code_rows // 16) * 16
    id_code = jnp.concatenate([in_ids // 128, in_ids % 128]).astype(jnp.bfloat16)
    id_code = jnp.pad(id_code, (0, code_rows * emb_width - 2 * slots))
    payload = jnp.concatenate([incoming, id_code.reshape(code_rows, emb_width)])
    def shift(x, step):
        return lax.ppermute(x, "rep", [(i, (i + step) % replicas) for i in range(replicas)])

    from_prev = shift(payload, 1)
    from_next = shift(payload, -1)
    half = payload.shape[0] // 2
    far_a = shift(from_prev[:half], 1)
    far_b = shift(from_next[half:], -1)

    def decode(code):
        code = code.reshape(-1)[: 2 * slots].astype(jnp.int32)
        return code[:slots] * 128 + code[slots:]

    rows_near = jnp.concatenate([from_prev[:slots], from_next[:slots]])
    keys_near = jnp.concatenate([decode(from_prev[slots:]), decode(from_next[slots:])])
    far_tail = slots - half
    rows_far = jnp.concatenate([far_a, far_b[:far_tail]])
    keys_far = decode(far_b[far_tail:])

    first_row = my_rep * share_rows
    share_ids = first_row + jnp.arange(share_rows, dtype=jnp.int32)
    look_cent = centroids[in_ids].astype(jnp.float32)
    own_cent = lax.dynamic_slice_in_dim(centroids, first_row, share_rows, 0).astype(jnp.float32)

    queries = jnp.concatenate([in_ids, share_ids])
    own_sums = match_sums(queries, in_ids, incoming)
    near_sums = match_sums(queries, keys_near, rows_near)
    look_sum = own_sums[:slots] + near_sums[:slots] + match_sums(in_ids, keys_far, rows_far)
    picked = normalize(look_cent + look_sum)
    returned = lax.all_to_all(picked, "wide", split_axis=0, concat_axis=0, tiled=True)

    share_sum = own_sums[slots:] + near_sums[slots:] + match_sums(share_ids, keys_far, rows_far)
    own_rows = normalize(own_cent + share_sum)

    gathered_rows = jnp.dot(place_bf.T, returned, preferred_element_type=jnp.float32)
    residuals = (embedded.astype(jnp.float32) - gathered_rows).astype(jnp.bfloat16)
    return (own_rows, residuals)


def solution(mesh):
    return jax.shard_map(
        body,
        mesh=mesh,
        in_specs=(P(("wide", "rep"), None), P(("wide", "rep")), P(), P(), P("wide", None)),
        out_specs=(P(("wide", "rep"), None), P(("wide", "rep"), None)),
        check_vma=False,
    )
```

```python
import jax
import jax.numpy as jnp
from jax import lax
from jax.sharding import PartitionSpec as P


def normalize(updated):
    return (
        updated * lax.rsqrt(jnp.mean(updated * updated, axis=-1, keepdims=True) + 1e-06)
    ).astype(jnp.bfloat16)


def match_sums(queries, keys, rows, block_rows=None):
    count = queries.shape[0]
    block_rows = block_rows or count
    padded = -(-count // block_rows) * block_rows
    blocks = jnp.pad(queries, (0, padded - count), constant_values=-1).reshape(-1, block_rows)

    def one_block(block_ids):
        selector = (block_ids[:, None] == keys[None, :]).astype(jnp.bfloat16)
        return jnp.dot(selector, rows, preferred_element_type=jnp.float32)

    return lax.map(one_block, blocks).reshape(padded, -1)[:count]


def body(passages, cluster_ids, w_first, w_second, centroids):
    tok_rows = passages.shape[0]
    owners = lax.axis_size("wide")
    replicas = lax.axis_size("rep")
    cent_rows = centroids.shape[0]
    share_rows = cent_rows // replicas
    capacity = 3 * tok_rows // owners
    slots = owners * capacity
    my_rep = lax.axis_index("rep")

    owner_of = cluster_ids // cent_rows
    local_id = cluster_ids - owner_of * cent_rows
    member = owner_of[:, None] == jnp.arange(owners, dtype=jnp.int32)[None, :]
    row = jnp.arange(tok_rows, dtype=jnp.int32)
    earlier = (row[:, None] > row[None, :]).astype(jnp.bfloat16)
    before = jnp.dot(earlier, member.astype(jnp.bfloat16), preferred_element_type=jnp.float32)
    slot_of = jnp.sum(jnp.where(member, before, 0.0), axis=1).astype(jnp.int32)
    target = owner_of * capacity + slot_of
    place = target[None, :] == jnp.arange(slots, dtype=jnp.int32)[:, None]
    place_bf = place.astype(jnp.bfloat16)
    out_ids = jnp.sum(jnp.where(place, local_id[None, :], 0), axis=1)

    hidden = jax.nn.gelu(
        jnp.dot(passages, w_first, preferred_element_type=jnp.float32), approximate=True
    ).astype(jnp.bfloat16)
    projected = jnp.dot(hidden, w_second, preferred_element_type=jnp.float32)
    embedded = (
        projected * lax.rsqrt(jnp.mean(projected * projected, axis=-1, keepdims=True) + 1e-06)
    ).astype(jnp.bfloat16)

    outgoing = jnp.dot(place_bf, embedded, preferred_element_type=jnp.float32).astype(jnp.bfloat16)
    emb_width = outgoing.shape[1]
    incoming = lax.all_to_all(outgoing, "wide", split_axis=0, concat_axis=0, tiled=True)
    in_ids = lax.all_to_all(out_ids, "wide", split_axis=0, concat_axis=0, tiled=True)

    half_rows = slots // 2
    code_rows = -(-2 * half_rows // emb_width)
    code_rows = -(-code_rows // 16) * 16

    def with_code(part):
        part_ids = in_ids[part * half_rows : (part + 1) * half_rows]
        id_code = jnp.concatenate([part_ids // 128, part_ids % 128]).astype(jnp.bfloat16)
        id_code = jnp.pad(id_code, (0, code_rows * emb_width - 2 * half_rows))
        return jnp.concatenate(
            [incoming[part * half_rows : (part + 1) * half_rows],
             id_code.reshape(code_rows, emb_width)]
        )

    def split(pieces):
        blocks = [piece[:half_rows] for piece in pieces]
        ids = []
        for piece in pieces:
            code = piece[half_rows:].reshape(-1)[: 2 * half_rows].astype(jnp.int32)
            ids.append(code[:half_rows] * 128 + code[half_rows:])
        return jnp.concatenate(ids), jnp.concatenate(blocks)

    def shift(x, step):
        return lax.ppermute(x, "rep", [(i, (i + step) % replicas) for i in range(replicas)])

    payload_a = with_code(0)
    prev_a = shift(payload_a, 1)
    next_a = shift(payload_a, -1)
    payload_b, _, _ = lax.optimization_barrier((with_code(1), prev_a, next_a))
    prev_b = shift(payload_b, 1)
    next_b = shift(payload_b, -1)
    far_a = shift(prev_a, 1)
    far_b = shift(next_b, -1)

    keys_a, near_a = split([prev_a, next_a])
    keys_b, near_b = split([prev_b, next_b])
    keys_far, far = split([far_a, far_b])

    first_row = my_rep * share_rows
    share_ids = first_row + jnp.arange(share_rows, dtype=jnp.int32)
    look_cent = centroids[in_ids]
    own_cent = lax.dynamic_slice_in_dim(centroids, first_row, share_rows, 0)

    queries = jnp.concatenate([in_ids, share_ids])
    own_sums = match_sums(queries, in_ids, incoming, queries.shape[0] // 2)
    sums_a = match_sums(queries, keys_a, near_a, queries.shape[0] // 2)
    sums_b = match_sums(queries, keys_b, near_b, queries.shape[0] // 2)
    look_sum = (own_sums[:slots] + sums_a[:slots] + sums_b[:slots]
                + match_sums(in_ids, keys_far, far, 1024))
    picked = normalize(look_cent.astype(jnp.float32) + look_sum)
    returned = lax.all_to_all(picked, "wide", split_axis=0, concat_axis=0, tiled=True)

    share_sum = (own_sums[slots:] + sums_a[slots:] + sums_b[slots:]
                 + match_sums(share_ids, keys_far, far, 1024))
    own_rows = normalize(own_cent.astype(jnp.float32) + share_sum)

    gathered_rows = jnp.dot(place_bf.T, returned, preferred_element_type=jnp.float32)
    residuals = (embedded.astype(jnp.float32) - gathered_rows).astype(jnp.bfloat16)
    return (own_rows, residuals)


def solution(mesh):
    return jax.shard_map(
        body,
        mesh=mesh,
        in_specs=(P(("wide", "rep"), None), P(("wide", "rep")), P(), P(), P("wide", None)),
        out_specs=(P(("wide", "rep"), None), P(("wide", "rep"), None)),
        check_vma=False,
    )
```

```python
import jax
import jax.numpy as jnp
from jax import lax
from jax.sharding import PartitionSpec as P


def normalize(updated):
    return (
        updated * lax.rsqrt(jnp.mean(updated * updated, axis=-1, keepdims=True) + 1e-06)
    ).astype(jnp.bfloat16)


def match_sums(queries, keys, rows, block_rows=None):
    count = queries.shape[0]
    block_rows = block_rows or count
    padded = -(-count // block_rows) * block_rows
    blocks = jnp.pad(queries, (0, padded - count), constant_values=-1).reshape(-1, block_rows)

    def one_block(block_ids):
        selector = (block_ids[:, None] == keys[None, :]).astype(jnp.bfloat16)
        return jnp.dot(selector, rows, preferred_element_type=jnp.float32)

    return lax.map(one_block, blocks).reshape(padded, -1)[:count]


def body(passages, cluster_ids, w_first, w_second, centroids):
    tok_rows = passages.shape[0]
    owners = lax.axis_size("wide")
    replicas = lax.axis_size("rep")
    cent_rows = centroids.shape[0]
    share_rows = cent_rows // replicas
    capacity = 3 * tok_rows // owners
    slots = owners * capacity
    my_rep = lax.axis_index("rep")

    owner_of = cluster_ids // cent_rows
    local_id = cluster_ids - owner_of * cent_rows
    member = owner_of[:, None] == jnp.arange(owners, dtype=jnp.int32)[None, :]
    row = jnp.arange(tok_rows, dtype=jnp.int32)
    earlier = (row[:, None] > row[None, :]).astype(jnp.bfloat16)
    before = jnp.dot(earlier, member.astype(jnp.bfloat16), preferred_element_type=jnp.float32)
    slot_of = jnp.sum(jnp.where(member, before, 0.0), axis=1).astype(jnp.int32)
    target = owner_of * capacity + slot_of
    place = target[None, :] == jnp.arange(slots, dtype=jnp.int32)[:, None]
    place_bf = place.astype(jnp.bfloat16)
    out_ids = jnp.sum(jnp.where(place, local_id[None, :], 0), axis=1)

    hidden = jax.nn.gelu(
        jnp.dot(passages, w_first, preferred_element_type=jnp.float32), approximate=True
    ).astype(jnp.bfloat16)
    projected = jnp.dot(hidden, w_second, preferred_element_type=jnp.float32)
    embedded = (
        projected * lax.rsqrt(jnp.mean(projected * projected, axis=-1, keepdims=True) + 1e-06)
    ).astype(jnp.bfloat16)

    outgoing = jnp.dot(place_bf, embedded, preferred_element_type=jnp.float32).astype(jnp.bfloat16)
    emb_width = outgoing.shape[1]
    incoming = lax.all_to_all(outgoing, "wide", split_axis=0, concat_axis=0, tiled=True)
    in_ids = lax.all_to_all(out_ids, "wide", split_axis=0, concat_axis=0, tiled=True)

    half_rows = slots // 2
    code_rows = -(-2 * half_rows // emb_width)
    code_rows = -(-code_rows // 16) * 16

    def with_code(part):
        part_ids = in_ids[part * half_rows : (part + 1) * half_rows]
        id_code = jnp.concatenate([part_ids // 128, part_ids % 128]).astype(jnp.bfloat16)
        id_code = jnp.pad(id_code, (0, code_rows * emb_width - 2 * half_rows))
        return jnp.concatenate(
            [incoming[part * half_rows : (part + 1) * half_rows],
             id_code.reshape(code_rows, emb_width)]
        )

    def split(pieces):
        blocks = [piece[:half_rows] for piece in pieces]
        ids = []
        for piece in pieces:
            code = piece[half_rows:].reshape(-1)[: 2 * half_rows].astype(jnp.int32)
            ids.append(code[:half_rows] * 128 + code[half_rows:])
        return jnp.concatenate(ids), jnp.concatenate(blocks)

    def shift(x, step):
        return lax.ppermute(x, "rep", [(i, (i + step) % replicas) for i in range(replicas)])

    payload_a = with_code(0)
    prev_a = shift(payload_a, 1)
    next_a = shift(payload_a, -1)
    payload_b, _, _ = lax.optimization_barrier((with_code(1), prev_a, next_a))
    prev_b = shift(payload_b, 1)
    next_b = shift(payload_b, -1)
    far_a = shift(prev_a, 1)
    far_b = shift(next_b, -1)

    keys_a, near_a = split([prev_a, next_a])
    keys_b, near_b = split([prev_b, next_b])
    keys_far, far = split([far_a, far_b])

    first_row = my_rep * share_rows
    share_ids = first_row + jnp.arange(share_rows, dtype=jnp.int32)
    look_cent = centroids[in_ids]
    own_cent = lax.dynamic_slice_in_dim(centroids, first_row, share_rows, 0)

    queries = jnp.concatenate([in_ids, share_ids])
    own_sums = match_sums(queries, in_ids, incoming, queries.shape[0] // 2)
    sums_a = match_sums(queries, keys_a, near_a, queries.shape[0] // 2)
    sums_b = match_sums(queries, keys_b, near_b, queries.shape[0] // 2)
    look_sum = (own_sums[:slots] + sums_a[:slots] + sums_b[:slots]
                + match_sums(in_ids, keys_far, far, 1024))
    picked = normalize(look_cent.astype(jnp.float32) + look_sum)
    returned = lax.all_to_all(picked, "wide", split_axis=0, concat_axis=0, tiled=True)

    share_sum = (own_sums[slots:] + sums_a[slots:] + sums_b[slots:]
                 + match_sums(share_ids, keys_far, far, share_rows // 2))
    own_rows = normalize(own_cent.astype(jnp.float32) + share_sum)

    gathered_rows = jnp.dot(place_bf.T, returned, preferred_element_type=jnp.float32)
    residuals = (embedded.astype(jnp.float32) - gathered_rows).astype(jnp.bfloat16)
    return (own_rows, residuals)


def solution(mesh):
    return jax.shard_map(
        body,
        mesh=mesh,
        in_specs=(P(("wide", "rep"), None), P(("wide", "rep")), P(), P(), P("wide", None)),
        out_specs=(P(("wide", "rep"), None), P(("wide", "rep"), None)),
        check_vma=False,
    )
```

```python
import jax
import jax.numpy as jnp
from jax import lax
from jax.sharding import PartitionSpec as P


def normalize(updated):
    return (
        updated * lax.rsqrt(jnp.mean(updated * updated, axis=-1, keepdims=True) + 1e-06)
    ).astype(jnp.bfloat16)


def match_sums(queries, keys, rows, block_rows=None):
    count = queries.shape[0]
    block_rows = block_rows or count
    padded = -(-count // block_rows) * block_rows
    blocks = jnp.pad(queries, (0, padded - count), constant_values=-1).reshape(-1, block_rows)

    def one_block(block_ids):
        selector = (block_ids[:, None] == keys[None, :]).astype(jnp.bfloat16)
        return jnp.dot(selector, rows, preferred_element_type=jnp.float32)

    return lax.map(one_block, blocks).reshape(padded, -1)[:count]


def body(passages, cluster_ids, w_first, w_second, centroids):
    tok_rows = passages.shape[0]
    owners = lax.axis_size("wide")
    replicas = lax.axis_size("rep")
    cent_rows = centroids.shape[0]
    share_rows = cent_rows // replicas
    capacity = 3 * tok_rows // owners
    slots = owners * capacity
    my_rep = lax.axis_index("rep")

    owner_of = cluster_ids // cent_rows
    local_id = cluster_ids - owner_of * cent_rows
    member = owner_of[:, None] == jnp.arange(owners, dtype=jnp.int32)[None, :]
    row = jnp.arange(tok_rows, dtype=jnp.int32)
    earlier = (row[:, None] > row[None, :]).astype(jnp.bfloat16)
    before = jnp.dot(earlier, member.astype(jnp.bfloat16), preferred_element_type=jnp.float32)
    slot_of = jnp.sum(jnp.where(member, before, 0.0), axis=1).astype(jnp.int32)
    target = owner_of * capacity + slot_of
    place = target[None, :] == jnp.arange(slots, dtype=jnp.int32)[:, None]
    place_bf = place.astype(jnp.bfloat16)
    out_ids = jnp.sum(jnp.where(place, local_id[None, :], 0), axis=1)

    hidden = jax.nn.gelu(
        jnp.dot(passages, w_first, preferred_element_type=jnp.float32), approximate=True
    ).astype(jnp.bfloat16)
    projected = jnp.dot(hidden, w_second, preferred_element_type=jnp.float32)
    embedded = (
        projected * lax.rsqrt(jnp.mean(projected * projected, axis=-1, keepdims=True) + 1e-06)
    ).astype(jnp.bfloat16)

    outgoing = jnp.dot(place_bf, embedded, preferred_element_type=jnp.float32).astype(jnp.bfloat16)
    emb_width = outgoing.shape[1]
    incoming = lax.all_to_all(outgoing, "wide", split_axis=0, concat_axis=0, tiled=True)
    in_ids = lax.all_to_all(out_ids, "wide", split_axis=0, concat_axis=0, tiled=True)

    half_rows = slots // 2
    code_rows = -(-2 * half_rows // emb_width)
    code_rows = -(-code_rows // 16) * 16

    def with_code(part):
        part_ids = in_ids[part * half_rows : (part + 1) * half_rows]
        id_code = jnp.concatenate([part_ids // 128, part_ids % 128]).astype(jnp.bfloat16)
        id_code = jnp.pad(id_code, (0, code_rows * emb_width - 2 * half_rows))
        return jnp.concatenate(
            [incoming[part * half_rows : (part + 1) * half_rows],
             id_code.reshape(code_rows, emb_width)]
        )

    def split(pieces):
        blocks = [piece[:half_rows] for piece in pieces]
        ids = []
        for piece in pieces:
            code = piece[half_rows:].reshape(-1)[: 2 * half_rows].astype(jnp.int32)
            ids.append(code[:half_rows] * 128 + code[half_rows:])
        return jnp.concatenate(ids), jnp.concatenate(blocks)

    def shift(x, step):
        return lax.ppermute(x, "rep", [(i, (i + step) % replicas) for i in range(replicas)])

    payload_a = with_code(0)
    prev_a = shift(payload_a, 1)
    next_a = shift(payload_a, -1)
    payload_b, _, _ = lax.optimization_barrier((with_code(1), prev_a, next_a))
    prev_b = shift(payload_b, 1)
    next_b = shift(payload_b, -1)
    far_a = shift(prev_a, 1)
    far_b = shift(next_b, -1)

    keys_a, near_a = split([prev_a, next_a])
    keys_b, near_b = split([prev_b, next_b])
    keys_far, far = split([far_a, far_b])

    first_row = my_rep * share_rows
    share_ids = first_row + jnp.arange(share_rows, dtype=jnp.int32)
    look_cent = centroids[in_ids]
    own_cent = lax.dynamic_slice_in_dim(centroids, first_row, share_rows, 0)

    queries = jnp.concatenate([in_ids, share_ids])
    own_sums = match_sums(queries, in_ids, incoming, queries.shape[0] // 2)
    sums_a = match_sums(queries, keys_a, near_a, queries.shape[0] // 2)
    sums_b = match_sums(queries, keys_b, near_b, queries.shape[0] // 2)
    look_sum = (own_sums[:slots] + sums_a[:slots] + sums_b[:slots]
                + match_sums(in_ids, keys_far, far, slots // 2))
    picked = normalize(look_cent.astype(jnp.float32) + look_sum)
    returned = lax.all_to_all(picked, "wide", split_axis=0, concat_axis=0, tiled=True)

    share_sum = (own_sums[slots:] + sums_a[slots:] + sums_b[slots:]
                 + match_sums(share_ids, keys_far, far, 1024))
    own_rows = normalize(own_cent.astype(jnp.float32) + share_sum)

    gathered_rows = jnp.dot(place_bf.T, returned, preferred_element_type=jnp.float32)
    residuals = (embedded.astype(jnp.float32) - gathered_rows).astype(jnp.bfloat16)
    return (own_rows, residuals)


def solution(mesh):
    return jax.shard_map(
        body,
        mesh=mesh,
        in_specs=(P(("wide", "rep"), None), P(("wide", "rep")), P(), P(), P("wide", None)),
        out_specs=(P(("wide", "rep"), None), P(("wide", "rep"), None)),
        check_vma=False,
    )
```

```python
import jax
import jax.numpy as jnp
from jax import lax
from jax.sharding import PartitionSpec as P


def normalize(updated):
    return (
        updated * lax.rsqrt(jnp.mean(updated * updated, axis=-1, keepdims=True) + 1e-06)
    ).astype(jnp.bfloat16)


def match_sums(queries, keys, rows, block_rows=None):
    count = queries.shape[0]
    block_rows = block_rows or count
    padded = -(-count // block_rows) * block_rows
    blocks = jnp.pad(queries, (0, padded - count), constant_values=-1).reshape(-1, block_rows)

    def one_block(block_ids):
        selector = (block_ids[:, None] == keys[None, :]).astype(jnp.bfloat16)
        return jnp.dot(selector, rows, preferred_element_type=jnp.float32)

    return lax.map(one_block, blocks).reshape(padded, -1)[:count]


def body(passages, cluster_ids, w_first, w_second, centroids):
    tok_rows = passages.shape[0]
    owners = lax.axis_size("wide")
    replicas = lax.axis_size("rep")
    cent_rows = centroids.shape[0]
    share_rows = cent_rows // replicas
    capacity = 3 * tok_rows // owners
    slots = owners * capacity
    my_rep = lax.axis_index("rep")

    owner_of = cluster_ids // cent_rows
    local_id = cluster_ids - owner_of * cent_rows
    member = owner_of[:, None] == jnp.arange(owners, dtype=jnp.int32)[None, :]
    row = jnp.arange(tok_rows, dtype=jnp.int32)
    earlier = (row[:, None] > row[None, :]).astype(jnp.bfloat16)
    before = jnp.dot(earlier, member.astype(jnp.bfloat16), preferred_element_type=jnp.float32)
    slot_of = jnp.sum(jnp.where(member, before, 0.0), axis=1).astype(jnp.int32)
    target = owner_of * capacity + slot_of
    place = target[None, :] == jnp.arange(slots, dtype=jnp.int32)[:, None]
    place_bf = place.astype(jnp.bfloat16)
    out_ids = jnp.sum(jnp.where(place, local_id[None, :], 0), axis=1)

    hidden = jax.nn.gelu(
        jnp.dot(passages, w_first, preferred_element_type=jnp.float32), approximate=True
    ).astype(jnp.bfloat16)
    projected = jnp.dot(hidden, w_second, preferred_element_type=jnp.float32)
    embedded = (
        projected * lax.rsqrt(jnp.mean(projected * projected, axis=-1, keepdims=True) + 1e-06)
    ).astype(jnp.bfloat16)

    outgoing = jnp.dot(place_bf, embedded, preferred_element_type=jnp.float32).astype(jnp.bfloat16)
    emb_width = outgoing.shape[1]
    incoming = lax.all_to_all(outgoing, "wide", split_axis=0, concat_axis=0, tiled=True)
    in_ids = lax.all_to_all(out_ids, "wide", split_axis=0, concat_axis=0, tiled=True)

    half_rows = slots // 2
    code_rows = -(-2 * half_rows // emb_width)
    code_rows = -(-code_rows // 16) * 16

    def with_code(part):
        part_ids = in_ids[part * half_rows : (part + 1) * half_rows]
        id_code = jnp.concatenate([part_ids // 128, part_ids % 128]).astype(jnp.bfloat16)
        id_code = jnp.pad(id_code, (0, code_rows * emb_width - 2 * half_rows))
        return jnp.concatenate(
            [incoming[part * half_rows : (part + 1) * half_rows],
             id_code.reshape(code_rows, emb_width)]
        )

    def split(pieces):
        blocks = [piece[:half_rows] for piece in pieces]
        ids = []
        for piece in pieces:
            code = piece[half_rows:].reshape(-1)[: 2 * half_rows].astype(jnp.int32)
            ids.append(code[:half_rows] * 128 + code[half_rows:])
        return jnp.concatenate(ids), jnp.concatenate(blocks)

    def shift(x, step):
        return lax.ppermute(x, "rep", [(i, (i + step) % replicas) for i in range(replicas)])

    payload_a = with_code(0)
    prev_a = shift(payload_a, 1)
    next_a = shift(payload_a, -1)
    payload_b, _, _ = lax.optimization_barrier((with_code(1), prev_a, next_a))
    prev_b = shift(payload_b, 1)
    next_b = shift(payload_b, -1)
    far_a = shift(prev_a, 1)
    far_b = shift(next_b, -1)

    keys_a, near_a = split([prev_a, next_a])
    keys_b, near_b = split([prev_b, next_b])
    keys_far, far = split([far_a, far_b])

    first_row = my_rep * share_rows
    share_ids = first_row + jnp.arange(share_rows, dtype=jnp.int32)
    look_cent = centroids[in_ids]
    own_cent = lax.dynamic_slice_in_dim(centroids, first_row, share_rows, 0)

    queries = jnp.concatenate([in_ids, share_ids])
    own_sums = match_sums(queries, in_ids, incoming, queries.shape[0] // 2)
    sums_a = match_sums(queries, keys_a, near_a, queries.shape[0] // 2)
    sums_b = match_sums(queries, keys_b, near_b, queries.shape[0] // 2)
    look_sum = (own_sums[:slots] + sums_a[:slots] + sums_b[:slots]
                + match_sums(in_ids, keys_far, far, slots))
    picked = normalize(look_cent.astype(jnp.float32) + look_sum)
    returned = lax.all_to_all(picked, "wide", split_axis=0, concat_axis=0, tiled=True)

    share_sum = (own_sums[slots:] + sums_a[slots:] + sums_b[slots:]
                 + match_sums(share_ids, keys_far, far, 1024))
    own_rows = normalize(own_cent.astype(jnp.float32) + share_sum)

    gathered_rows = jnp.dot(place_bf.T, returned, preferred_element_type=jnp.float32)
    residuals = (embedded.astype(jnp.float32) - gathered_rows).astype(jnp.bfloat16)
    return (own_rows, residuals)


def solution(mesh):
    return jax.shard_map(
        body,
        mesh=mesh,
        in_specs=(P(("wide", "rep"), None), P(("wide", "rep")), P(), P(), P("wide", None)),
        out_specs=(P(("wide", "rep"), None), P(("wide", "rep"), None)),
        check_vma=False,
    )
```

```python
import jax
import jax.numpy as jnp
from jax import lax
from jax.sharding import PartitionSpec as P


def normalize(updated):
    return (
        updated * lax.rsqrt(jnp.mean(updated * updated, axis=-1, keepdims=True) + 1e-06)
    ).astype(jnp.bfloat16)


def match_sums(queries, keys, rows, block_rows=None):
    count = queries.shape[0]
    block_rows = block_rows or count
    padded = -(-count // block_rows) * block_rows
    blocks = jnp.pad(queries, (0, padded - count), constant_values=-1).reshape(-1, block_rows)

    def one_block(block_ids):
        selector = (block_ids[:, None] == keys[None, :]).astype(jnp.bfloat16)
        return jnp.dot(selector, rows, preferred_element_type=jnp.float32)

    return lax.map(one_block, blocks).reshape(padded, -1)[:count]


def body(passages, cluster_ids, w_first, w_second, centroids):
    tok_rows = passages.shape[0]
    owners = lax.axis_size("wide")
    replicas = lax.axis_size("rep")
    cent_rows = centroids.shape[0]
    share_rows = cent_rows // replicas
    capacity = 3 * tok_rows // owners
    slots = owners * capacity
    my_rep = lax.axis_index("rep")

    owner_of = cluster_ids // cent_rows
    local_id = cluster_ids - owner_of * cent_rows
    member = owner_of[:, None] == jnp.arange(owners, dtype=jnp.int32)[None, :]
    row = jnp.arange(tok_rows, dtype=jnp.int32)
    earlier = (row[:, None] > row[None, :]).astype(jnp.bfloat16)
    before = jnp.dot(earlier, member.astype(jnp.bfloat16), preferred_element_type=jnp.float32)
    slot_of = jnp.sum(jnp.where(member, before, 0.0), axis=1).astype(jnp.int32)
    target = owner_of * capacity + slot_of
    place = target[None, :] == jnp.arange(slots, dtype=jnp.int32)[:, None]
    place_bf = place.astype(jnp.bfloat16)
    out_ids = jnp.sum(jnp.where(place, local_id[None, :], 0), axis=1)

    hidden = jax.nn.gelu(
        jnp.dot(passages, w_first, preferred_element_type=jnp.float32), approximate=True
    ).astype(jnp.bfloat16)
    projected = jnp.dot(hidden, w_second, preferred_element_type=jnp.float32)
    embedded = (
        projected * lax.rsqrt(jnp.mean(projected * projected, axis=-1, keepdims=True) + 1e-06)
    ).astype(jnp.bfloat16)

    outgoing = jnp.dot(place_bf, embedded, preferred_element_type=jnp.float32).astype(jnp.bfloat16)
    emb_width = outgoing.shape[1]
    incoming = lax.all_to_all(outgoing, "wide", split_axis=0, concat_axis=0, tiled=True)
    in_ids = lax.all_to_all(out_ids, "wide", split_axis=0, concat_axis=0, tiled=True)

    half_rows = slots // 2
    code_rows = -(-2 * half_rows // emb_width)
    code_rows = -(-code_rows // 16) * 16

    def with_code(part):
        part_ids = in_ids[part * half_rows : (part + 1) * half_rows]
        id_code = jnp.concatenate([part_ids // 128, part_ids % 128]).astype(jnp.bfloat16)
        id_code = jnp.pad(id_code, (0, code_rows * emb_width - 2 * half_rows))
        return jnp.concatenate(
            [incoming[part * half_rows : (part + 1) * half_rows],
             id_code.reshape(code_rows, emb_width)]
        )

    def split(pieces):
        blocks = [piece[:half_rows] for piece in pieces]
        ids = []
        for piece in pieces:
            code = piece[half_rows:].reshape(-1)[: 2 * half_rows].astype(jnp.int32)
            ids.append(code[:half_rows] * 128 + code[half_rows:])
        return jnp.concatenate(ids), jnp.concatenate(blocks)

    def shift(x, step):
        return lax.ppermute(x, "rep", [(i, (i + step) % replicas) for i in range(replicas)])

    payload_a = with_code(0)
    prev_a = shift(payload_a, 1)
    next_a = shift(payload_a, -1)
    payload_b, _, _ = lax.optimization_barrier((with_code(1), prev_a, next_a))
    prev_b = shift(payload_b, 1)
    next_b = shift(payload_b, -1)
    far_a = shift(prev_a, 1)
    far_b = shift(next_b, -1)

    keys_a, near_a = split([prev_a, next_a])
    keys_b, near_b = split([prev_b, next_b])
    keys_far, far = split([far_a, far_b])

    first_row = my_rep * share_rows
    share_ids = first_row + jnp.arange(share_rows, dtype=jnp.int32)
    look_cent = centroids[in_ids]
    own_cent = lax.dynamic_slice_in_dim(centroids, first_row, share_rows, 0)

    queries = jnp.concatenate([in_ids, share_ids])
    own_sums = match_sums(queries, in_ids, incoming, queries.shape[0] // 2)
    sums_a = match_sums(queries, keys_a, near_a, queries.shape[0] // 2)
    sums_b = match_sums(queries, keys_b, near_b, queries.shape[0] // 2)
    look_sum = (own_sums[:slots] + sums_a[:slots] + sums_b[:slots]
                + match_sums(in_ids, keys_far, far, slots))
    picked = normalize(look_cent.astype(jnp.float32) + look_sum)
    returned = lax.all_to_all(picked, "wide", split_axis=0, concat_axis=0, tiled=True)

    share_sum = (own_sums[slots:] + sums_a[slots:] + sums_b[slots:]
                 + match_sums(share_ids, keys_far, far, share_rows // 2))
    own_rows = normalize(own_cent.astype(jnp.float32) + share_sum)

    gathered_rows = jnp.dot(place_bf.T, returned, preferred_element_type=jnp.float32)
    residuals = (embedded.astype(jnp.float32) - gathered_rows).astype(jnp.bfloat16)
    return (own_rows, residuals)


def solution(mesh):
    return jax.shard_map(
        body,
        mesh=mesh,
        in_specs=(P(("wide", "rep"), None), P(("wide", "rep")), P(), P(), P("wide", None)),
        out_specs=(P(("wide", "rep"), None), P(("wide", "rep"), None)),
        check_vma=False,
    )
```
